32 devices in a mesh: pool: 8 (over z, x), tp: 4 (over y, core).
Axes of the slice: x: 2, y: 2, z: 4, core: 2. Of those that a mesh axis runs over, the one named last changes fastest.
Arguments:
- draft_states: bfloat16 [1024, 8192], P(None, 'pool'), may hold values from -12 to 12
- w_qkv: bfloat16 [8192, 10240], P('pool', 'tp'), may hold values from -0.0625 to 0.0625
- w_out: bfloat16 [8192, 8192], P('tp', 'pool'), may hold values from -0.0625 to 0.0625
- kv_pool: bfloat16 [640, 128, 2048], P('pool', None, 'tp'), may hold values from -58 to 58
- resident_kv: bfloat16 [16, 8, 128, 2048], P('pool', None, None, 'tp'), may hold values from -58 to 58
- page_owner: int32 [16, 32], replicated, may hold values from 0 to 7, as said below
- page_slot: int32 [16, 32], replicated, may hold values from 0 to 79, as said below
- hist_len: int32 [16], replicated, may hold values from 3073 to 4096, as said below
- res_count: int32 [16], replicated, may hold values from 0 to 8, as said below
- parents: int32 [16, 64], replicated, may hold values from -1 to 62, as said below
Outputs:
- layer_out: bfloat16 [1024, 8192], P('tp', 'pool')
The draws below stay inside these ranges and needn't reach their ends.
Inputs may be any that keep to these rules, and one draw needn't show every extreme that they name: `page_owner`: among the 64 entries of the users of one pool index, one owner is named 16 times, one owner is never named, and every other owner 16 / 2 times; each owner is the most named one for exactly one pool index. No pair (page_owner, page_slot) is named twice. `hist_len`: some user's history has exactly 4096 tokens. res_count[u] is at most the page count ceil(hist_len[u] / 128) of user u; some user has exactly 8. parents[u, i] lies between i - 4 and i - 1 and is -1 where that is negative; parents[u, 0] = -1 and parents[u, 63] = 62.
All inputs are finite; a program needn't handle non-finite values.
Results may differ from the reference program's by a relative error of at most 0.013.
The reference program's roundings to bfloat16 on the way count: a program that leaves them out, or rounds other values in their place, can miss the bound.
Values may be sent and summed in bfloat16 or wider, within the bound.
No kernel may reach another device: no remote copies, remote signals or barrier semaphores. Data moves between devices by JAX's collectives and lax.ppermute only.
A program may use at most 192 MiB of HBM per device.

```python
import math
import jax
import jax.numpy as jnp
from jax import lax

D = 8192
H = 64
KVH = 8
HD = 128
DRAFT = 64
PAGE = 128
MAXP = 32
MAXRES = 8
USER_DEV = 2
USERS = 16
TOKENS = 1024
PAGES_DEV = 80
MAXLEN = 4096
QKV = 10240
N_POOL = 8


def kv_values(key, shape):
    column = lax.broadcasted_iota(jnp.int32, shape, len(shape) - 1)
    is_key = column % (2 * HD) < HD
    base_values = jnp.clip(jax.random.normal(key, shape, jnp.float32), -6.0, 6.0)
    boost = jnp.ones(shape[:-1], jnp.float32)
    factor = jnp.where(is_key, 0.75 * boost[..., None], 8.0)
    return (base_values * factor).astype(jnp.bfloat16)


def draw_kv_pool(key, part):
    return kv_values(key, (N_POOL * PAGES_DEV, PAGE, 2 * KVH * HD))


def draw_resident_kv(key, part):
    return kv_values(key, (USERS, MAXRES, PAGE, 2 * KVH * HD))


def permute_small(subkey):
    return jax.random.permutation(subkey, N_POOL - 1)


def permute_block(subkey):
    return jax.random.permutation(subkey, USER_DEV * MAXP)


def page_table(key):
    block_rows = USER_DEV * MAXP
    shift = jax.random.randint(jax.random.fold_in(key, 1), (), 0, N_POOL)
    hottest = (jnp.arange(N_POOL) + shift) % N_POOL
    orders = jax.vmap(permute_small)(jax.random.split(jax.random.fold_in(key, 2), N_POOL))
    ranking = jnp.concatenate([hottest[:, None], (hottest[:, None] + 1 + orders) % N_POOL], 1)
    column = jnp.arange(block_rows) % N_POOL
    column = jnp.where(column < 2, 0, column)
    owner_seq = ranking[:, column]
    shuffles = jax.vmap(permute_block)(jax.random.split(jax.random.fold_in(key, 3), N_POOL))
    owners = jnp.take_along_axis(owner_seq, shuffles, 1).reshape(USERS, MAXP)
    flat_owner = owners.reshape(-1)
    one_hot = (flat_owner[:, None] == jnp.arange(N_POOL)[None, :]).astype(jnp.int32)
    slot_ranks = jnp.sum((jnp.cumsum(one_hot, 0) - one_hot) * one_hot, 1)
    offsets = jax.random.randint(jax.random.fold_in(key, 4), (N_POOL,), 0, PAGES_DEV)
    offsets = jnp.where(jnp.arange(N_POOL) == hottest[0], PAGES_DEV - 1, offsets)
    slots = ((slot_ranks + offsets[flat_owner]) % PAGES_DEV).reshape(USERS, MAXP)
    return (owners.astype(jnp.int32), slots.astype(jnp.int32))


def draw_page_owner(key, part):
    return page_table(jax.random.fold_in(key, 11))[0]


def draw_page_slot(key, part):
    return page_table(jax.random.fold_in(key, 11))[1]


def user_table(key):
    lengths = jax.random.randint(jax.random.fold_in(key, 1), (USERS,), MAXLEN - MAXLEN // 4 + 1, MAXLEN + 1)
    longest = jax.random.randint(jax.random.fold_in(key, 2), (), 0, USERS)
    is_longest = jnp.arange(USERS) == longest
    lengths = jnp.where(is_longest, MAXLEN, lengths)
    page_counts = (lengths + PAGE - 1) // PAGE
    resident = jax.random.randint(jax.random.fold_in(key, 3), (USERS,), 0, MAXRES + 1)
    resident = jnp.minimum(resident, page_counts)
    resident = jnp.where(is_longest, MAXRES, resident)
    return (lengths.astype(jnp.int32), resident.astype(jnp.int32))


def draw_hist_len(key, part):
    return user_table(jax.random.fold_in(key, 7))[0]


def draw_res_count(key, part):
    return user_table(jax.random.fold_in(key, 7))[1]


def draw_parents(key, part):
    backward = jax.random.randint(key, (USERS, DRAFT), 0, 4)
    backward = jnp.where(jnp.arange(DRAFT)[None, :] == DRAFT - 1, 0, backward)
    return jnp.maximum(jnp.arange(DRAFT)[None, :] - 1 - backward, -1).astype(jnp.int32)


def spiked(drawn, stream_key, source, target, blocks, factor):
    def block_of(position):
        return (jnp.arange(drawn.shape[position]) // (drawn.shape[position] // blocks)).reshape((-1,) + (1,) * (drawn.ndim - 1 - position))

    one_side = jax.random.permutation(stream_key, blocks)[block_of(target)]
    second = (block_of(target) + blocks // 2) % blocks
    return jnp.where((block_of(source) == one_side) | (block_of(source) == second), factor * drawn, drawn)


def steps_of(own_key, shape, cuts, least, largest):
    level = 1.0
    for dim, shards_of in cuts:
        draws = jax.random.uniform(jax.random.fold_in(jax.random.fold_in(own_key, 6), dim), (shards_of,), jnp.float32, least / len(cuts), largest / len(cuts))
        level = level * jnp.repeat(jnp.exp(draws), shape[dim] // shards_of).reshape((-1,) + (1,) * (len(shape) - 1 - dim))
    return level


def scatter_about(own_key, shape, spread, reach, cuts=(), kind=jnp.bfloat16):
    entries = jax.random.normal(own_key, shape, jnp.float32) * spread
    if len(cuts) > 0:
        entries = steps_of(own_key, shape, cuts, -0.22, 0.18) * entries
    return jnp.clip(entries, min=-reach, max=reach).astype(kind)


def bell_draw_with(own_key, extent, spread, most, cuts, heavy, held_as=jnp.bfloat16):
    result = spread * jax.random.normal(own_key, extent, jnp.float32)
    if cuts:
        result = result * steps_of(own_key, extent, cuts, -0.22, 0.18)
    return jnp.clip(spiked(result, jax.random.fold_in(own_key, 3), *heavy), -most, most).astype(held_as)


def setup_inputs(seed: int = 0) -> dict:
    streams_of = jax.random.split(jax.random.key(seed), 11)
    return {
        "draft_states": bell_draw_with(streams_of[0], (TOKENS, D), 2.0, 12.0, ((1, 8),), (1, 0, 8, 2.0)),
        "w_qkv": scatter_about(streams_of[1], (D, QKV), D ** -0.5, 0.0625, ((0, 8), (1, 4))),
        "w_out": scatter_about(streams_of[2], (H * HD, D), (H * HD) ** -0.5, 0.0625, ((0, 4), (1, 8))),
        "kv_pool": draw_kv_pool(jax.random.fold_in(streams_of[10], 71), 0),
        "resident_kv": draw_resident_kv(jax.random.fold_in(streams_of[10], 71), 0),
        "page_owner": draw_page_owner(jax.random.fold_in(streams_of[10], 71), 0),
        "page_slot": draw_page_slot(jax.random.fold_in(streams_of[10], 71), 0),
        "hist_len": draw_hist_len(jax.random.fold_in(streams_of[10], 71), 0),
        "res_count": draw_res_count(jax.random.fold_in(streams_of[10], 71), 0),
        "parents": draw_parents(jax.random.fold_in(streams_of[10], 71), 0),
    }


ROPE_BASE = 500000.0


def ancestry_of(parents):
    users_count, draft_len = parents.shape

    def visit_token(step_index, ancestry):
        parent_ids = parents[:, step_index]
        parent_rows = ancestry[jnp.arange(users_count), jnp.maximum(parent_ids, 0)]
        own_row = (jnp.arange(draft_len) == step_index).astype(jnp.float32)
        new_row = own_row[None, :] + jnp.where((parent_ids >= 0)[:, None], parent_rows, 0.0)
        return ancestry.at[:, step_index, :].set(new_row)

    return lax.fori_loop(0, draft_len, visit_token, jnp.zeros((users_count, draft_len, draft_len), jnp.float32))


def rotate(vectors, positions):
    half_size = vectors.shape[-1] // 2
    frequencies = jnp.exp(jnp.arange(half_size).astype(jnp.float32) * (-2.0 * math.log(ROPE_BASE) / vectors.shape[-1]))
    angles = positions[..., None] * frequencies
    cosines = jnp.cos(angles)
    sines = jnp.sin(angles)
    lower_half = vectors[..., :half_size]
    upper_half = vectors[..., half_size:]
    return jnp.concatenate([lower_half * cosines - upper_half * sines, upper_half * cosines + lower_half * sines], -1)


def reference(draft_states, w_qkv, w_out, kv_pool, resident_kv, page_owner, page_slot, hist_len, res_count, parents):
    group_size = H // KVH
    projected = jnp.dot(draft_states, w_qkv, preferred_element_type=jnp.float32).reshape(USERS, DRAFT, KVH, group_size + 2, HD)
    ancestry = ancestry_of(parents)
    positions = hist_len.astype(jnp.float32)[:, None] + jnp.sum(ancestry, -1) - 1.0
    queries = lax.optimization_barrier(rotate(projected[:, :, :, :group_size], positions[:, :, None, None]).astype(jnp.bfloat16))
    draft_key = lax.optimization_barrier(rotate(projected[:, :, :, group_size], positions[:, :, None]).astype(jnp.bfloat16))
    draft_value = lax.optimization_barrier(projected[:, :, :, group_size + 1].astype(jnp.bfloat16))
    score_scale = HD ** -0.5
    numbers = jnp.arange(MAXP)
    token_place = jnp.arange(MAXP * PAGE)

    def attend_user(user):
        global_page = page_owner[user] * PAGES_DEV + page_slot[user]
        from_pool = kv_pool[global_page]
        from_cache = resident_kv[user][jnp.minimum(numbers, MAXRES - 1)]
        history = jnp.where((numbers < res_count[user])[:, None, None], from_cache, from_pool)
        history = history.reshape(MAXP * PAGE, KVH, 2, HD).astype(jnp.float32)
        user_queries = queries[user].astype(jnp.float32)
        hist_scores = jnp.einsum("tkgd,skd->tkgs", user_queries, history[:, :, 0]) * score_scale
        draft_scores = jnp.einsum("tkgd,jkd->tkgj", user_queries, draft_key[user].astype(jnp.float32)) * score_scale
        hist_ok = (token_place < hist_len[user])[None, None, None, :]
        draft_ok = (ancestry[user] > 0.5)[:, None, None, :]
        row_max = jnp.maximum(jnp.max(jnp.where(hist_ok, hist_scores, -jnp.inf), -1),
                              jnp.max(jnp.where(draft_ok, draft_scores, -jnp.inf), -1))
        hist_weight = jnp.where(hist_ok, jnp.exp(hist_scores - row_max[..., None]), 0.0)
        draft_weight = jnp.where(draft_ok, jnp.exp(draft_scores - row_max[..., None]), 0.0)
        denominator = jnp.sum(hist_weight, -1) + jnp.sum(draft_weight, -1)
        hist_prob = lax.optimization_barrier(hist_weight.astype(jnp.bfloat16)).astype(jnp.float32)
        draft_prob = lax.optimization_barrier(draft_weight.astype(jnp.bfloat16)).astype(jnp.float32)
        weighted = jnp.einsum("tkgs,skd->tkgd", hist_prob, history[:, :, 1])
        weighted = weighted + jnp.einsum("tkgj,jkd->tkgd", draft_prob, draft_value[user].astype(jnp.float32))
        return (weighted / denominator[..., None]).astype(jnp.bfloat16)

    attention = lax.map(attend_user, jnp.arange(USERS)).reshape(USERS * DRAFT, H * HD)
    return jnp.dot(attention, w_out, preferred_element_type=jnp.float32).astype(jnp.bfloat16)
```

```python
import math

import jax
import jax.numpy as jnp
from jax import lax
from jax.sharding import PartitionSpec as P

H = 64
KVH = 8
HD = 128
DRAFT = 64
PAGE = 128
MAXP = 32
MAXRES = 8
USER_DEV = 2


ROPE_BASE = 500000.0


def ancestry_of(parents):
    users_count, draft_len = parents.shape
    tokens = jnp.arange(draft_len)
    reach = (parents[:, :, None] == tokens[None, None, :]).astype(jnp.float32)
    reach = reach + (tokens[:, None] == tokens[None, :]).astype(jnp.float32)[None]
    for unused in range(max(1, math.ceil(math.log2(draft_len)))):
        reach = jnp.minimum(
            jnp.einsum(
                "uij,ujk->uik",
                reach.astype(jnp.bfloat16),
                reach.astype(jnp.bfloat16),
                preferred_element_type=jnp.float32,
            ),
            1.0,
        )
    return reach


def rotate(vectors, positions):
    half_size = vectors.shape[-1] // 2
    frequencies = jnp.exp(
        jnp.arange(half_size).astype(jnp.float32) * (-2.0 * math.log(ROPE_BASE) / vectors.shape[-1])
    )
    angles = positions[..., None] * frequencies
    cosines = jnp.cos(angles)
    sines = jnp.sin(angles)
    lower_half = vectors[..., :half_size]
    upper_half = vectors[..., half_size:]
    return jnp.concatenate(
        [lower_half * cosines - upper_half * sines, upper_half * cosines + lower_half * sines], -1
    )


def attend_dense(queries, history, draft_key, draft_value, visible, length):
    heads_kv, row_count, head_dim = queries.shape
    score_scale = head_dim ** (-0.5)
    hist_scores = (
        jnp.einsum("krd,skd->krs", queries, history[:, :, 0], preferred_element_type=jnp.float32)
        * score_scale
    )
    draft_scores = (
        jnp.einsum("krd,jkd->krj", queries, draft_key, preferred_element_type=jnp.float32)
        * score_scale
    )
    hist_ok = (jnp.arange(history.shape[0]) < length)[None, None, :]
    draft_ok = visible[None]
    row_max = jnp.maximum(
        jnp.max(jnp.where(hist_ok, hist_scores, -jnp.inf), -1),
        jnp.max(jnp.where(draft_ok, draft_scores, -jnp.inf), -1),
    )
    hist_weight = jnp.where(hist_ok, jnp.exp(hist_scores - row_max[..., None]), 0.0)
    draft_weight = jnp.where(draft_ok, jnp.exp(draft_scores - row_max[..., None]), 0.0)
    denominator = jnp.sum(hist_weight, -1) + jnp.sum(draft_weight, -1)
    weighted = jnp.einsum(
        "krs,skd->krd",
        hist_weight.astype(jnp.bfloat16),
        history[:, :, 1],
        preferred_element_type=jnp.float32,
    ) + jnp.einsum(
        "krj,jkd->krd",
        draft_weight.astype(jnp.bfloat16),
        draft_value,
        preferred_element_type=jnp.float32,
    )
    return weighted / denominator[..., None]


def finish(result, draft_len):
    heads_kv, row_count, head_dim = result.shape
    result = result.reshape(heads_kv, draft_len, row_count // draft_len, head_dim).transpose(
        1, 0, 2, 3
    )
    return result.reshape(draft_len, heads_kv * row_count // draft_len * head_dim).astype(
        jnp.bfloat16
    )


def body(
    draft_states,
    w_qkv,
    w_out,
    kv_pool,
    resident_kv,
    page_owner,
    page_slot,
    hist_len,
    res_count,
    parents,
):
    pool_size = lax.axis_size("pool")
    my_index = lax.axis_index("pool")
    group_size = H // KVH
    local_cols = w_qkv.shape[1]
    heads_kv = local_cols // ((group_size + 2) * HD)
    projected = lax.psum_scatter(
        jnp.dot(draft_states, w_qkv, preferred_element_type=jnp.float32),
        "pool",
        scatter_dimension=0,
        tiled=True,
    )
    projected = projected.reshape(USER_DEV, DRAFT, heads_kv, group_size + 2, HD)
    first_user = my_index * USER_DEV
    my_lengths = lax.dynamic_slice_in_dim(hist_len, first_user, USER_DEV)
    my_resident = lax.dynamic_slice_in_dim(res_count, first_user, USER_DEV)
    my_parents = lax.dynamic_slice_in_dim(parents, first_user, USER_DEV, 0)
    ancestry = ancestry_of(my_parents)
    positions = my_lengths.astype(jnp.float32)[:, None] + jnp.sum(ancestry, -1) - 1.0
    queries = rotate(projected[:, :, :, :group_size], positions[:, :, None, None]).astype(
        jnp.bfloat16
    )
    draft_key = rotate(projected[:, :, :, group_size], positions[:, :, None]).astype(jnp.bfloat16)
    draft_value = projected[:, :, :, group_size + 1].astype(jnp.bfloat16)
    row_count = DRAFT * group_size
    query_rows = queries.transpose(0, 2, 1, 3, 4).reshape(USER_DEV, heads_kv, row_count, HD)
    visible = jnp.repeat(ancestry > 0.5, group_size, axis=1)
    block_rows = USER_DEV * MAXP
    capacity = 2 * block_rows // pool_size
    kv_cols = kv_pool.shape[2]
    owner_blocks = page_owner.reshape(pool_size, block_rows)
    slot_blocks = page_slot.reshape(pool_size, block_rows)
    one_hot = (owner_blocks[:, :, None] == jnp.arange(pool_size)[None, None, :]).astype(jnp.int32)
    slot_ranks = jnp.sum((jnp.cumsum(one_hot, axis=1) - one_hot) * one_hot, axis=2)
    targets = jnp.arange(pool_size)[:, None] * capacity + slot_ranks
    send_to = jnp.where(owner_blocks == my_index, targets, pool_size * capacity).reshape(-1)
    pack_index = (
        jnp.zeros((pool_size * capacity,), jnp.int32)
        .at[send_to]
        .set(slot_blocks.reshape(-1), mode="drop")
    )
    local_source = resident_kv.reshape(USER_DEV * MAXRES, PAGE, kv_cols)
    outputs = []
    packed = kv_pool[pack_index]
    arrived = lax.all_to_all(packed, "pool", split_axis=0, concat_axis=0, tiled=True)
    my_owner = lax.dynamic_index_in_dim(owner_blocks, my_index, 0, keepdims=False).reshape(
        USER_DEV, MAXP
    )
    my_rank = lax.dynamic_index_in_dim(slot_ranks, my_index, 0, keepdims=False).reshape(
        USER_DEV, MAXP
    )
    numbers = jnp.arange(MAXP)
    for local_user in range(USER_DEV):
        resident_pages = local_source[local_user * MAXRES + jnp.minimum(numbers, MAXRES - 1)]
        pool_pages = arrived[my_owner[local_user] * capacity + my_rank[local_user]]
        history = jnp.where(
            (numbers < my_resident[local_user])[:, None, None], resident_pages, pool_pages
        ).reshape(MAXP * PAGE, heads_kv, 2, HD)
        result = attend_dense(
            query_rows[local_user],
            history,
            draft_key[local_user],
            draft_value[local_user],
            visible[local_user],
            my_lengths[local_user],
        )
        outputs.append(finish(result, DRAFT))
    attention = jnp.concatenate(outputs, 0)
    partial_out = jnp.dot(
        lax.all_gather(attention, "pool", axis=0, tiled=True),
        w_out,
        preferred_element_type=jnp.float32,
    )
    return lax.psum_scatter(partial_out.astype(jnp.bfloat16), "tp", scatter_dimension=0, tiled=True)


def solution(mesh):
    in_specs = (
        P(None, "pool"),
        P("pool", "tp"),
        P("tp", "pool"),
        P("pool", None, "tp"),
        P("pool", None, None, "tp"),
        P(),
        P(),
        P(),
        P(),
        P(),
    )
    out_specs = P("tp", "pool")
    return jax.shard_map(body, mesh=mesh, in_specs=in_specs, out_specs=out_specs, check_vma=False)
```

```python
import math

import jax
import jax.numpy as jnp
from jax import lax
from jax.sharding import PartitionSpec as P

H = 64
KVH = 8
HD = 128
DRAFT = 64
PAGE = 128
MAXP = 32
MAXRES = 8
USER_DEV = 2


ROPE_BASE = 500000.0


def ancestry_of(parents):
    users_count, draft_len = parents.shape
    tokens = jnp.arange(draft_len)
    reach = (parents[:, :, None] == tokens[None, None, :]).astype(jnp.float32)
    reach = reach + (tokens[:, None] == tokens[None, :]).astype(jnp.float32)[None]
    for unused in range(max(1, math.ceil(math.log2(draft_len)))):
        reach = jnp.minimum(
            jnp.einsum(
                "uij,ujk->uik",
                reach.astype(jnp.bfloat16),
                reach.astype(jnp.bfloat16),
                preferred_element_type=jnp.float32,
            ),
            1.0,
        )
    return reach


def rotate(vectors, positions):
    half_size = vectors.shape[-1] // 2
    frequencies = jnp.exp(
        jnp.arange(half_size).astype(jnp.float32) * (-2.0 * math.log(ROPE_BASE) / vectors.shape[-1])
    )
    angles = positions[..., None] * frequencies
    cosines = jnp.cos(angles)
    sines = jnp.sin(angles)
    lower_half = vectors[..., :half_size]
    upper_half = vectors[..., half_size:]
    return jnp.concatenate(
        [lower_half * cosines - upper_half * sines, upper_half * cosines + lower_half * sines], -1
    )


def attend_dense(queries, history, draft_key, draft_value, visible, length):
    heads_kv, row_count, head_dim = queries.shape
    score_scale = head_dim ** (-0.5)
    hist_ok = (jnp.arange(history.shape[0]) < length)[None, :]
    results = []
    for head in range(heads_kv):
        keys = history[:, 2 * head * head_dim : (2 * head + 1) * head_dim]
        values = history[:, (2 * head + 1) * head_dim : (2 * head + 2) * head_dim]
        hist_scores = (
            jnp.einsum("rd,sd->rs", queries[head], keys, preferred_element_type=jnp.float32)
            * score_scale
        )
        draft_scores = (
            jnp.einsum(
                "rd,jd->rj", queries[head], draft_key[:, head], preferred_element_type=jnp.float32
            )
            * score_scale
        )
        row_max = jnp.maximum(
            jnp.max(jnp.where(hist_ok, hist_scores, -jnp.inf), -1),
            jnp.max(jnp.where(visible, draft_scores, -jnp.inf), -1),
        )
        hist_weight = jnp.where(hist_ok, jnp.exp(hist_scores - row_max[:, None]), 0.0)
        draft_weight = jnp.where(visible, jnp.exp(draft_scores - row_max[:, None]), 0.0)
        denominator = jnp.sum(hist_weight, -1) + jnp.sum(draft_weight, -1)
        weighted = jnp.einsum(
            "rs,sd->rd",
            hist_weight.astype(jnp.bfloat16),
            values,
            preferred_element_type=jnp.float32,
        ) + jnp.einsum(
            "rj,jd->rd",
            draft_weight.astype(jnp.bfloat16),
            draft_value[:, head],
            preferred_element_type=jnp.float32,
        )
        results.append(weighted / denominator[:, None])
    return jnp.stack(results, 0)


def finish(result, draft_len):
    heads_kv, row_count, head_dim = result.shape
    result = result.reshape(heads_kv, draft_len, row_count // draft_len, head_dim).transpose(
        1, 0, 2, 3
    )
    return result.reshape(draft_len, heads_kv * row_count // draft_len * head_dim).astype(
        jnp.bfloat16
    )


def body(
    draft_states,
    w_qkv,
    w_out,
    kv_pool,
    resident_kv,
    page_owner,
    page_slot,
    hist_len,
    res_count,
    parents,
):
    pool_size = lax.axis_size("pool")
    my_index = lax.axis_index("pool")
    group_size = H // KVH
    local_cols = w_qkv.shape[1]
    heads_kv = local_cols // ((group_size + 2) * HD)
    projected = lax.psum_scatter(
        jnp.dot(draft_states, w_qkv, preferred_element_type=jnp.float32),
        "pool",
        scatter_dimension=0,
        tiled=True,
    )
    projected = projected.reshape(USER_DEV, DRAFT, heads_kv, group_size + 2, HD)
    first_user = my_index * USER_DEV
    my_lengths = lax.dynamic_slice_in_dim(hist_len, first_user, USER_DEV)
    my_resident = lax.dynamic_slice_in_dim(res_count, first_user, USER_DEV)
    my_parents = lax.dynamic_slice_in_dim(parents, first_user, USER_DEV, 0)
    ancestry = ancestry_of(my_parents)
    positions = my_lengths.astype(jnp.float32)[:, None] + jnp.sum(ancestry, -1) - 1.0
    queries = rotate(projected[:, :, :, :group_size], positions[:, :, None, None]).astype(
        jnp.bfloat16
    )
    draft_key = rotate(projected[:, :, :, group_size], positions[:, :, None]).astype(jnp.bfloat16)
    draft_value = projected[:, :, :, group_size + 1].astype(jnp.bfloat16)
    row_count = DRAFT * group_size
    query_rows = queries.transpose(0, 2, 1, 3, 4).reshape(USER_DEV, heads_kv, row_count, HD)
    visible = jnp.repeat(ancestry > 0.5, group_size, axis=1)
    block_rows = USER_DEV * MAXP
    capacity = block_rows // pool_size
    kv_cols = kv_pool.shape[2]
    owner_blocks = page_owner.reshape(pool_size, block_rows)
    slot_blocks = page_slot.reshape(pool_size, block_rows)
    one_hot = (owner_blocks[:, :, None] == jnp.arange(pool_size)[None, None, :]).astype(jnp.int32)
    slot_ranks = jnp.sum((jnp.cumsum(one_hot, axis=1) - one_hot) * one_hot, axis=2)
    hot_owner = jnp.argmax(jnp.sum(one_hot, axis=1), axis=1)
    mine = owner_blocks == my_index
    targets = jnp.arange(pool_size)[:, None] * capacity + slot_ranks
    send_to = jnp.where(mine & (slot_ranks < capacity), targets, pool_size * capacity)
    pack_index = (
        jnp.zeros((pool_size * capacity,), jnp.int32)
        .at[send_to.reshape(-1)]
        .set(slot_blocks.reshape(-1), mode="drop")
    )
    extra_to = jnp.where(mine & (slot_ranks >= capacity), slot_ranks - capacity, capacity)
    extra_index = (
        jnp.zeros((capacity,), jnp.int32)
        .at[extra_to.reshape(-1)]
        .set(slot_blocks.reshape(-1), mode="drop")
    )
    piece_rows = capacity * PAGE // pool_size
    arrived = lax.all_to_all(
        kv_pool[pack_index], "pool", split_axis=0, concat_axis=0, tiled=True
    )
    spread = lax.all_to_all(
        kv_pool[extra_index].reshape(pool_size, piece_rows, kv_cols),
        "pool",
        split_axis=0,
        concat_axis=0,
        tiled=True,
    )
    extra = lax.all_to_all(
        spread[hot_owner], "pool", split_axis=0, concat_axis=0, tiled=True
    ).reshape(capacity, PAGE, kv_cols)
    local_source = resident_kv.reshape(USER_DEV * MAXRES, PAGE, kv_cols)
    outputs = []
    my_owner = lax.dynamic_index_in_dim(owner_blocks, my_index, 0, keepdims=False).reshape(
        USER_DEV, MAXP
    )
    my_rank = lax.dynamic_index_in_dim(slot_ranks, my_index, 0, keepdims=False).reshape(
        USER_DEV, MAXP
    )
    numbers = jnp.arange(MAXP)
    for local_user in range(USER_DEV):
        owner = my_owner[local_user]
        rank = my_rank[local_user]
        resident_pages = local_source[local_user * MAXRES + jnp.minimum(numbers, MAXRES - 1)]
        regular_pages = arrived[owner * capacity + jnp.minimum(rank, capacity - 1)]
        extra_pages = extra[jnp.clip(rank - capacity, 0, capacity - 1)]
        history = jnp.where(
            (numbers < my_resident[local_user])[:, None, None],
            resident_pages,
            jnp.where((rank < capacity)[:, None, None], regular_pages, extra_pages),
        ).reshape(MAXP * PAGE, kv_cols)
        result = attend_dense(
            query_rows[local_user],
            history,
            draft_key[local_user],
            draft_value[local_user],
            visible[local_user],
            my_lengths[local_user],
        )
        outputs.append(finish(result, DRAFT))
    attention = jnp.concatenate(outputs, 0)
    partial_out = jnp.dot(
        lax.all_gather(attention, "pool", axis=0, tiled=True),
        w_out,
        preferred_element_type=jnp.float32,
    )
    return lax.psum_scatter(partial_out.astype(jnp.bfloat16), "tp", scatter_dimension=0, tiled=True)


def solution(mesh):
    in_specs = (
        P(None, "pool"),
        P("pool", "tp"),
        P("tp", "pool"),
        P("pool", None, "tp"),
        P("pool", None, None, "tp"),
        P(),
        P(),
        P(),
        P(),
        P(),
    )
    out_specs = P("tp", "pool")
    return jax.shard_map(body, mesh=mesh, in_specs=in_specs, out_specs=out_specs, check_vma=False)
```

```python
import math

import jax
import jax.numpy as jnp
from jax import lax
from jax.sharding import PartitionSpec as P

H = 64
KVH = 8
HD = 128
DRAFT = 64
PAGE = 128
MAXP = 32
MAXRES = 8
USER_DEV = 2


ROPE_BASE = 500000.0


def ancestry_of(parents):
    users_count, draft_len = parents.shape
    tokens = jnp.arange(draft_len)
    reach = (parents[:, :, None] == tokens[None, None, :]).astype(jnp.float32)
    reach = reach + (tokens[:, None] == tokens[None, :]).astype(jnp.float32)[None]
    for unused in range(max(1, math.ceil(math.log2(draft_len)))):
        reach = jnp.minimum(
            jnp.einsum(
                "uij,ujk->uik",
                reach.astype(jnp.bfloat16),
                reach.astype(jnp.bfloat16),
                preferred_element_type=jnp.float32,
            ),
            1.0,
        )
    return reach


def rotate(vectors, positions):
    half_size = vectors.shape[-1] // 2
    frequencies = jnp.exp(
        jnp.arange(half_size).astype(jnp.float32) * (-2.0 * math.log(ROPE_BASE) / vectors.shape[-1])
    )
    angles = positions[..., None] * frequencies
    cosines = jnp.cos(angles)
    sines = jnp.sin(angles)
    lower_half = vectors[..., :half_size]
    upper_half = vectors[..., half_size:]
    return jnp.concatenate(
        [lower_half * cosines - upper_half * sines, upper_half * cosines + lower_half * sines], -1
    )


def attend_dense(queries, history, draft_key, draft_value, visible, length):
    heads_kv, row_count, head_dim = queries.shape
    score_scale = head_dim ** (-0.5)
    hist_ok = (jnp.arange(history.shape[0]) < length)[None, :]
    results = []
    for head in range(heads_kv):
        keys = history[:, 2 * head * head_dim : (2 * head + 1) * head_dim]
        values = history[:, (2 * head + 1) * head_dim : (2 * head + 2) * head_dim]
        hist_scores = (
            jnp.einsum("rd,sd->rs", queries[head], keys, preferred_element_type=jnp.float32)
            * score_scale
        )
        draft_scores = (
            jnp.einsum(
                "rd,jd->rj", queries[head], draft_key[:, head], preferred_element_type=jnp.float32
            )
            * score_scale
        )
        row_max = jnp.maximum(
            jnp.max(jnp.where(hist_ok, hist_scores, -jnp.inf), -1),
            jnp.max(jnp.where(visible, draft_scores, -jnp.inf), -1),
        )
        hist_weight = jnp.where(hist_ok, jnp.exp(hist_scores - row_max[:, None]), 0.0)
        draft_weight = jnp.where(visible, jnp.exp(draft_scores - row_max[:, None]), 0.0)
        denominator = jnp.sum(hist_weight, -1) + jnp.sum(draft_weight, -1)
        weighted = jnp.einsum(
            "rs,sd->rd",
            hist_weight.astype(jnp.bfloat16),
            values,
            preferred_element_type=jnp.float32,
        ) + jnp.einsum(
            "rj,jd->rd",
            draft_weight.astype(jnp.bfloat16),
            draft_value[:, head],
            preferred_element_type=jnp.float32,
        )
        results.append(weighted / denominator[:, None])
    return jnp.stack(results, 0)


def finish(result, draft_len):
    heads_kv, row_count, head_dim = result.shape
    result = result.reshape(heads_kv, draft_len, row_count // draft_len, head_dim).transpose(
        1, 0, 2, 3
    )
    return result.reshape(draft_len, heads_kv * row_count // draft_len * head_dim).astype(
        jnp.bfloat16
    )


def body(
    draft_states,
    w_qkv,
    w_out,
    kv_pool,
    resident_kv,
    page_owner,
    page_slot,
    hist_len,
    res_count,
    parents,
):
    pool_size = lax.axis_size("pool")
    my_index = lax.axis_index("pool")
    group_size = H // KVH
    local_cols = w_qkv.shape[1]
    heads_kv = local_cols // ((group_size + 2) * HD)
    projected = lax.psum_scatter(
        jnp.dot(draft_states, w_qkv, preferred_element_type=jnp.float32),
        "pool",
        scatter_dimension=0,
        tiled=True,
    )
    projected = projected.reshape(USER_DEV, DRAFT, heads_kv, group_size + 2, HD)
    first_user = my_index * USER_DEV
    my_lengths = lax.dynamic_slice_in_dim(hist_len, first_user, USER_DEV)
    my_resident = lax.dynamic_slice_in_dim(res_count, first_user, USER_DEV)
    my_parents = lax.dynamic_slice_in_dim(parents, first_user, USER_DEV, 0)
    ancestry = ancestry_of(my_parents)
    positions = my_lengths.astype(jnp.float32)[:, None] + jnp.sum(ancestry, -1) - 1.0
    queries = rotate(projected[:, :, :, :group_size], positions[:, :, None, None]).astype(
        jnp.bfloat16
    )
    draft_key = rotate(projected[:, :, :, group_size], positions[:, :, None]).astype(jnp.bfloat16)
    draft_value = projected[:, :, :, group_size + 1].astype(jnp.bfloat16)
    row_count = DRAFT * group_size
    query_rows = queries.transpose(0, 2, 1, 3, 4).reshape(USER_DEV, heads_kv, row_count, HD)
    visible = jnp.repeat(ancestry > 0.5, group_size, axis=1)
    block_rows = USER_DEV * MAXP
    capacity = block_rows // pool_size
    kv_cols = kv_pool.shape[2]
    owner_blocks = page_owner.reshape(pool_size, block_rows)
    slot_blocks = page_slot.reshape(pool_size, block_rows)
    one_hot = (owner_blocks[:, :, None] == jnp.arange(pool_size)[None, None, :]).astype(jnp.int32)
    slot_ranks = jnp.sum((jnp.cumsum(one_hot, axis=1) - one_hot) * one_hot, axis=2)
    hot_owner = jnp.argmax(jnp.sum(one_hot, axis=1), axis=1)
    mine = owner_blocks == my_index
    targets = jnp.arange(pool_size)[:, None] * capacity + slot_ranks
    send_to = jnp.where(mine & (slot_ranks < capacity), targets, pool_size * capacity)
    pack_index = (
        jnp.zeros((pool_size * capacity,), jnp.int32)
        .at[send_to.reshape(-1)]
        .set(slot_blocks.reshape(-1), mode="drop")
    )
    extra_to = jnp.where(mine & (slot_ranks >= capacity), slot_ranks - capacity, capacity)
    extra_index = (
        jnp.zeros((capacity,), jnp.int32)
        .at[extra_to.reshape(-1)]
        .set(slot_blocks.reshape(-1), mode="drop")
    )
    piece_rows = capacity * PAGE // pool_size
    outgoing = jnp.concatenate(
        [
            kv_pool[pack_index].reshape(pool_size, capacity * PAGE, kv_cols),
            kv_pool[extra_index].reshape(pool_size, piece_rows, kv_cols),
        ],
        1,
    )
    incoming = lax.all_to_all(outgoing, "pool", split_axis=0, concat_axis=0, tiled=True)
    arrived = incoming[:, : capacity * PAGE].reshape(pool_size * capacity, PAGE, kv_cols)
    spread = incoming[:, capacity * PAGE :]
    extra = lax.all_to_all(
        spread[hot_owner], "pool", split_axis=0, concat_axis=0, tiled=True
    ).reshape(capacity, PAGE, kv_cols)
    local_source = resident_kv.reshape(USER_DEV * MAXRES, PAGE, kv_cols)
    outputs = []
    my_owner = lax.dynamic_index_in_dim(owner_blocks, my_index, 0, keepdims=False).reshape(
        USER_DEV, MAXP
    )
    my_rank = lax.dynamic_index_in_dim(slot_ranks, my_index, 0, keepdims=False).reshape(
        USER_DEV, MAXP
    )
    numbers = jnp.arange(MAXP)
    for local_user in range(USER_DEV):
        owner = my_owner[local_user]
        rank = my_rank[local_user]
        resident_pages = local_source[local_user * MAXRES + jnp.minimum(numbers, MAXRES - 1)]
        regular_pages = arrived[owner * capacity + jnp.minimum(rank, capacity - 1)]
        extra_pages = extra[jnp.clip(rank - capacity, 0, capacity - 1)]
        history = jnp.where(
            (numbers < my_resident[local_user])[:, None, None],
            resident_pages,
            jnp.where((rank < capacity)[:, None, None], regular_pages, extra_pages),
        ).reshape(MAXP * PAGE, kv_cols)
        result = attend_dense(
            query_rows[local_user],
            history,
            draft_key[local_user],
            draft_value[local_user],
            visible[local_user],
            my_lengths[local_user],
        )
        outputs.append(finish(result, DRAFT))
    attention = jnp.concatenate(outputs, 0)
    partial_out = jnp.dot(
        lax.all_gather(attention, "pool", axis=0, tiled=True),
        w_out,
        preferred_element_type=jnp.float32,
    )
    return lax.psum_scatter(partial_out.astype(jnp.bfloat16), "tp", scatter_dimension=0, tiled=True)


def solution(mesh):
    in_specs = (
        P(None, "pool"),
        P("pool", "tp"),
        P("tp", "pool"),
        P("pool", None, "tp"),
        P("pool", None, None, "tp"),
        P(),
        P(),
        P(),
        P(),
        P(),
    )
    out_specs = P("tp", "pool")
    return jax.shard_map(body, mesh=mesh, in_specs=in_specs, out_specs=out_specs, check_vma=False)
```

```python
import math

import jax
import jax.numpy as jnp
from jax import lax
from jax.sharding import PartitionSpec as P

H = 64
KVH = 8
HD = 128
DRAFT = 64
PAGE = 128
MAXP = 32
MAXRES = 8
USER_DEV = 2


ROPE_BASE = 500000.0


def ancestry_of(parents):
    users_count, draft_len = parents.shape
    tokens = jnp.arange(draft_len)
    reach = (parents[:, :, None] == tokens[None, None, :]).astype(jnp.float32)
    reach = reach + (tokens[:, None] == tokens[None, :]).astype(jnp.float32)[None]
    for unused in range(max(1, math.ceil(math.log2(draft_len)))):
        reach = jnp.minimum(
            jnp.einsum(
                "uij,ujk->uik",
                reach.astype(jnp.bfloat16),
                reach.astype(jnp.bfloat16),
                preferred_element_type=jnp.float32,
            ),
            1.0,
        )
    return reach


def rotate(vectors, positions):
    half_size = vectors.shape[-1] // 2
    frequencies = jnp.exp(
        jnp.arange(half_size).astype(jnp.float32) * (-2.0 * math.log(ROPE_BASE) / vectors.shape[-1])
    )
    angles = positions[..., None] * frequencies
    cosines = jnp.cos(angles)
    sines = jnp.sin(angles)
    lower_half = vectors[..., :half_size]
    upper_half = vectors[..., half_size:]
    return jnp.concatenate(
        [lower_half * cosines - upper_half * sines, upper_half * cosines + lower_half * sines], -1
    )


def attend_dense(queries, history, draft_key, draft_value, visible, lengths):
    users, heads_kv, row_count, head_dim = queries.shape
    score_scale = head_dim ** (-0.5)
    hist_ok = (jnp.arange(history.shape[1])[None, :] < lengths[:, None])[:, None, :]
    results = []
    for head in range(heads_kv):
        keys = history[:, :, 2 * head * head_dim : (2 * head + 1) * head_dim]
        values = history[:, :, (2 * head + 1) * head_dim : (2 * head + 2) * head_dim]
        hist_scores = (
            jnp.einsum(
                "urd,usd->urs", queries[:, head], keys, preferred_element_type=jnp.float32
            )
            * score_scale
        )
        draft_scores = (
            jnp.einsum(
                "urd,ujd->urj",
                queries[:, head],
                draft_key[:, :, head],
                preferred_element_type=jnp.float32,
            )
            * score_scale
        )
        row_max = jnp.maximum(
            jnp.max(jnp.where(hist_ok, hist_scores, -jnp.inf), -1),
            jnp.max(jnp.where(visible, draft_scores, -jnp.inf), -1),
        )
        hist_weight = jnp.where(hist_ok, jnp.exp(hist_scores - row_max[..., None]), 0.0)
        draft_weight = jnp.where(visible, jnp.exp(draft_scores - row_max[..., None]), 0.0)
        denominator = jnp.sum(hist_weight, -1) + jnp.sum(draft_weight, -1)
        weighted = jnp.einsum(
            "urs,usd->urd",
            hist_weight.astype(jnp.bfloat16),
            values,
            preferred_element_type=jnp.float32,
        ) + jnp.einsum(
            "urj,ujd->urd",
            draft_weight.astype(jnp.bfloat16),
            draft_value[:, :, head],
            preferred_element_type=jnp.float32,
        )
        results.append(weighted / denominator[..., None])
    return jnp.stack(results, 1)


def finish(result, draft_len):
    users, heads_kv, row_count, head_dim = result.shape
    result = result.reshape(users, heads_kv, draft_len, row_count // draft_len, head_dim)
    return (
        result.transpose(0, 2, 1, 3, 4)
        .reshape(users * draft_len, heads_kv * row_count // draft_len * head_dim)
        .astype(jnp.bfloat16)
    )


def body(
    draft_states,
    w_qkv,
    w_out,
    kv_pool,
    resident_kv,
    page_owner,
    page_slot,
    hist_len,
    res_count,
    parents,
):
    pool_size = lax.axis_size("pool")
    my_index = lax.axis_index("pool")
    group_size = H // KVH
    local_cols = w_qkv.shape[1]
    heads_kv = local_cols // ((group_size + 2) * HD)
    partial_projection = jnp.dot(draft_states, w_qkv, preferred_element_type=jnp.float32)
    partial_projection, page_owner, page_slot = lax.optimization_barrier(
        (partial_projection, page_owner, page_slot)
    )
    projected = lax.psum_scatter(
        partial_projection,
        "pool",
        scatter_dimension=0,
        tiled=True,
    )
    projected = projected.reshape(USER_DEV, DRAFT, heads_kv, group_size + 2, HD)
    first_user = my_index * USER_DEV
    my_lengths = lax.dynamic_slice_in_dim(hist_len, first_user, USER_DEV)
    my_resident = lax.dynamic_slice_in_dim(res_count, first_user, USER_DEV)
    my_parents = lax.dynamic_slice_in_dim(parents, first_user, USER_DEV, 0)
    ancestry = ancestry_of(my_parents)
    positions = my_lengths.astype(jnp.float32)[:, None] + jnp.sum(ancestry, -1) - 1.0
    queries = rotate(projected[:, :, :, :group_size], positions[:, :, None, None]).astype(
        jnp.bfloat16
    )
    draft_key = rotate(projected[:, :, :, group_size], positions[:, :, None]).astype(jnp.bfloat16)
    draft_value = projected[:, :, :, group_size + 1].astype(jnp.bfloat16)
    row_count = DRAFT * group_size
    query_rows = queries.transpose(0, 2, 1, 3, 4).reshape(USER_DEV, heads_kv, row_count, HD)
    visible = jnp.repeat(ancestry > 0.5, group_size, axis=1)
    block_rows = USER_DEV * MAXP
    capacity = block_rows // pool_size
    kv_cols = kv_pool.shape[2]
    owner_blocks = page_owner.reshape(pool_size, block_rows)
    slot_blocks = page_slot.reshape(pool_size, block_rows)
    one_hot = (owner_blocks[:, :, None] == jnp.arange(pool_size)[None, None, :]).astype(jnp.int32)
    slot_ranks = jnp.sum((jnp.cumsum(one_hot, axis=1) - one_hot) * one_hot, axis=2)
    hot_owner = jnp.argmax(jnp.sum(one_hot, axis=1), axis=1)
    mine = owner_blocks == my_index
    targets = jnp.arange(pool_size)[:, None] * capacity + slot_ranks
    send_to = jnp.where(mine & (slot_ranks < capacity), targets, pool_size * capacity)
    pack_index = (
        jnp.zeros((pool_size * capacity,), jnp.int32)
        .at[send_to.reshape(-1)]
        .set(slot_blocks.reshape(-1), mode="drop")
    )
    extra_to = jnp.where(mine & (slot_ranks >= capacity), slot_ranks - capacity, capacity)
    extra_index = (
        jnp.zeros((capacity,), jnp.int32)
        .at[extra_to.reshape(-1)]
        .set(slot_blocks.reshape(-1), mode="drop")
    )
    piece_rows = capacity * PAGE // pool_size
    arrived = lax.all_to_all(
        kv_pool[pack_index], "pool", split_axis=0, concat_axis=0, tiled=True
    )
    spread = lax.all_to_all(
        kv_pool[extra_index].reshape(pool_size, piece_rows, kv_cols),
        "pool",
        split_axis=0,
        concat_axis=0,
        tiled=True,
    )
    extra = lax.all_to_all(
        spread[hot_owner], "pool", split_axis=0, concat_axis=0, tiled=True
    ).reshape(capacity, PAGE, kv_cols)
    local_source = resident_kv.reshape(USER_DEV * MAXRES, PAGE, kv_cols)
    my_owner = lax.dynamic_index_in_dim(owner_blocks, my_index, 0, keepdims=False).reshape(
        USER_DEV, MAXP
    )
    my_rank = lax.dynamic_index_in_dim(slot_ranks, my_index, 0, keepdims=False).reshape(
        USER_DEV, MAXP
    )
    numbers = jnp.arange(MAXP)
    user_ids = jnp.arange(USER_DEV)[:, None]
    resident_pages = local_source[user_ids * MAXRES + jnp.minimum(numbers, MAXRES - 1)[None, :]]
    regular_pages = arrived[my_owner * capacity + jnp.minimum(my_rank, capacity - 1)]
    extra_pages = extra[jnp.clip(my_rank - capacity, 0, capacity - 1)]
    history = jnp.where(
        (numbers[None, :] < my_resident[:, None])[:, :, None, None],
        resident_pages,
        jnp.where((my_rank < capacity)[:, :, None, None], regular_pages, extra_pages),
    ).reshape(USER_DEV, MAXP * PAGE, kv_cols)
    attention = finish(
        attend_dense(query_rows, history, draft_key, draft_value, visible, my_lengths), DRAFT
    )
    partial_out = jnp.dot(
        lax.all_gather(attention, "pool", axis=0, tiled=True),
        w_out,
        preferred_element_type=jnp.float32,
    )
    return lax.psum_scatter(partial_out.astype(jnp.bfloat16), "tp", scatter_dimension=0, tiled=True)


def solution(mesh):
    in_specs = (
        P(None, "pool"),
        P("pool", "tp"),
        P("tp", "pool"),
        P("pool", None, "tp"),
        P("pool", None, None, "tp"),
        P(),
        P(),
        P(),
        P(),
        P(),
    )
    out_specs = P("tp", "pool")
    return jax.shard_map(body, mesh=mesh, in_specs=in_specs, out_specs=out_specs, check_vma=False)
```

```python
import math

import jax
import jax.numpy as jnp
from jax import lax
from jax.sharding import PartitionSpec as P

H = 64
KVH = 8
HD = 128
DRAFT = 64
PAGE = 128
MAXP = 32
MAXRES = 8
USER_DEV = 2


ROPE_BASE = 500000.0


def ancestry_of(parents):
    users_count, draft_len = parents.shape
    tokens = jnp.arange(draft_len)
    reach = (parents[:, :, None] == tokens[None, None, :]).astype(jnp.float32)
    reach = reach + (tokens[:, None] == tokens[None, :]).astype(jnp.float32)[None]
    for unused in range(max(1, math.ceil(math.log2(draft_len)))):
        reach = jnp.minimum(
            jnp.einsum(
                "uij,ujk->uik",
                reach.astype(jnp.bfloat16),
                reach.astype(jnp.bfloat16),
                preferred_element_type=jnp.float32,
            ),
            1.0,
        )
    return reach


def rotate(vectors, positions):
    half_size = vectors.shape[-1] // 2
    frequencies = jnp.exp(
        jnp.arange(half_size).astype(jnp.float32) * (-2.0 * math.log(ROPE_BASE) / vectors.shape[-1])
    )
    angles = positions[..., None] * frequencies
    cosines = jnp.cos(angles)
    sines = jnp.sin(angles)
    lower_half = vectors[..., :half_size]
    upper_half = vectors[..., half_size:]
    return jnp.concatenate(
        [lower_half * cosines - upper_half * sines, upper_half * cosines + lower_half * sines], -1
    )


def attend_dense(queries, history, draft_key, draft_value, visible, length):
    heads_kv, row_count, head_dim = queries.shape
    score_scale = head_dim ** (-0.5)
    hist_ok = (jnp.arange(history.shape[0]) < length)[None, :]
    results = []
    for head in range(heads_kv):
        keys = history[:, 2 * head * head_dim : (2 * head + 1) * head_dim]
        values = history[:, (2 * head + 1) * head_dim : (2 * head + 2) * head_dim]
        hist_scores = (
            jnp.einsum("rd,sd->rs", queries[head], keys, preferred_element_type=jnp.float32)
            * score_scale
        )
        draft_scores = (
            jnp.einsum(
                "rd,jd->rj", queries[head], draft_key[:, head], preferred_element_type=jnp.float32
            )
            * score_scale
        )
        row_max = jnp.maximum(
            jnp.max(jnp.where(hist_ok, hist_scores, -jnp.inf), -1),
            jnp.max(jnp.where(visible, draft_scores, -jnp.inf), -1),
        )
        hist_weight = jnp.where(hist_ok, jnp.exp(hist_scores - row_max[:, None]), 0.0)
        draft_weight = jnp.where(visible, jnp.exp(draft_scores - row_max[:, None]), 0.0)
        denominator = jnp.sum(hist_weight, -1) + jnp.sum(draft_weight, -1)
        weighted = jnp.einsum(
            "rs,sd->rd",
            hist_weight.astype(jnp.bfloat16),
            values,
            preferred_element_type=jnp.float32,
        ) + jnp.einsum(
            "rj,jd->rd",
            draft_weight.astype(jnp.bfloat16),
            draft_value[:, head],
            preferred_element_type=jnp.float32,
        )
        results.append(weighted / denominator[:, None])
    return jnp.stack(results, 0)


def finish(result, draft_len):
    heads_kv, row_count, head_dim = result.shape
    result = result.reshape(heads_kv, draft_len, row_count // draft_len, head_dim).transpose(
        1, 0, 2, 3
    )
    return result.reshape(draft_len, heads_kv * row_count // draft_len * head_dim).astype(
        jnp.bfloat16
    )


def body(
    draft_states,
    w_qkv,
    w_out,
    kv_pool,
    resident_kv,
    page_owner,
    page_slot,
    hist_len,
    res_count,
    parents,
):
    pool_size = lax.axis_size("pool")
    my_index = lax.axis_index("pool")
    group_size = H // KVH
    local_cols = w_qkv.shape[1]
    heads_kv = local_cols // ((group_size + 2) * HD)
    projected = lax.psum_scatter(
        jnp.dot(draft_states, w_qkv, preferred_element_type=jnp.float32),
        "pool",
        scatter_dimension=0,
        tiled=True,
    )
    projected = projected.reshape(USER_DEV, DRAFT, heads_kv, group_size + 2, HD)
    first_user = my_index * USER_DEV
    my_lengths = lax.dynamic_slice_in_dim(hist_len, first_user, USER_DEV)
    my_resident = lax.dynamic_slice_in_dim(res_count, first_user, USER_DEV)
    my_parents = lax.dynamic_slice_in_dim(parents, first_user, USER_DEV, 0)
    ancestry = ancestry_of(my_parents)
    positions = my_lengths.astype(jnp.float32)[:, None] + jnp.sum(ancestry, -1) - 1.0
    queries = rotate(projected[:, :, :, :group_size], positions[:, :, None, None]).astype(
        jnp.bfloat16
    )
    draft_key = rotate(projected[:, :, :, group_size], positions[:, :, None]).astype(jnp.bfloat16)
    draft_value = projected[:, :, :, group_size + 1].astype(jnp.bfloat16)
    row_count = DRAFT * group_size
    query_rows = queries.transpose(0, 2, 1, 3, 4).reshape(USER_DEV, heads_kv, row_count, HD)
    visible = jnp.repeat(ancestry > 0.5, group_size, axis=1)
    block_rows = USER_DEV * MAXP
    capacity = block_rows // pool_size
    kv_cols = kv_pool.shape[2]
    owner_blocks = page_owner.reshape(pool_size, block_rows)
    slot_blocks = page_slot.reshape(pool_size, block_rows)
    one_hot = (owner_blocks[:, :, None] == jnp.arange(pool_size)[None, None, :]).astype(jnp.int32)
    slot_ranks = jnp.sum((jnp.cumsum(one_hot, axis=1) - one_hot) * one_hot, axis=2)
    hot_owner = jnp.argmax(jnp.sum(one_hot, axis=1), axis=1)
    mine = owner_blocks == my_index
    targets = jnp.arange(pool_size)[:, None] * capacity + slot_ranks
    send_to = jnp.where(mine & (slot_ranks < capacity), targets, pool_size * capacity)
    pack_index = (
        jnp.zeros((pool_size * capacity,), jnp.int32)
        .at[send_to.reshape(-1)]
        .set(slot_blocks.reshape(-1), mode="drop")
    )
    extra_to = jnp.where(mine & (slot_ranks >= capacity), slot_ranks - capacity, capacity)
    extra_index = (
        jnp.zeros((capacity,), jnp.int32)
        .at[extra_to.reshape(-1)]
        .set(slot_blocks.reshape(-1), mode="drop")
    )
    piece_rows = capacity * PAGE // pool_size
    arrived = lax.all_to_all(
        kv_pool[pack_index], "pool", split_axis=0, concat_axis=0, tiled=True
    )
    spread = lax.all_to_all(
        kv_pool[extra_index].reshape(pool_size, piece_rows, kv_cols),
        "pool",
        split_axis=0,
        concat_axis=0,
        tiled=True,
    )
    extra = lax.all_to_all(
        spread[hot_owner], "pool", split_axis=0, concat_axis=0, tiled=True
    ).reshape(capacity, PAGE, kv_cols)
    local_source = resident_kv.reshape(USER_DEV * MAXRES, PAGE, kv_cols)
    my_owner = lax.dynamic_index_in_dim(owner_blocks, my_index, 0, keepdims=False).reshape(
        USER_DEV, MAXP
    )
    my_rank = lax.dynamic_index_in_dim(slot_ranks, my_index, 0, keepdims=False).reshape(
        USER_DEV, MAXP
    )
    numbers = jnp.arange(MAXP)

    def attend_user(operands):
        local_user, owner, rank, resident, user_queries, user_key, user_value, seen, length = operands
        resident_pages = local_source[local_user * MAXRES + jnp.minimum(numbers, MAXRES - 1)]
        regular_pages = arrived[owner * capacity + jnp.minimum(rank, capacity - 1)]
        extra_pages = extra[jnp.clip(rank - capacity, 0, capacity - 1)]
        history = jnp.where(
            (numbers < resident)[:, None, None],
            resident_pages,
            jnp.where((rank < capacity)[:, None, None], regular_pages, extra_pages),
        ).reshape(MAXP * PAGE, kv_cols)
        result = attend_dense(user_queries, history, user_key, user_value, seen, length)
        return finish(result, DRAFT)

    attention = lax.map(
        attend_user,
        (
            jnp.arange(USER_DEV),
            my_owner,
            my_rank,
            my_resident,
            query_rows,
            draft_key,
            draft_value,
            visible,
            my_lengths,
        ),
    ).reshape(USER_DEV * DRAFT, -1)
    partial_out = jnp.dot(
        lax.all_gather(attention, "pool", axis=0, tiled=True),
        w_out,
        preferred_element_type=jnp.float32,
    )
    return halving_sum(partial_out, "tp").astype(jnp.bfloat16)


def halving_sum(partial, axis_name):
    size = lax.axis_size(axis_name)
    me = lax.axis_index(axis_name)
    rows = partial.shape[0] // size
    cols = partial.shape[1]
    held = partial
    bit = 1
    while bit < size:
        blocks = held.shape[0] // rows
        grouped = held.reshape(blocks // 2, 2, rows, cols)
        mine = (me // bit) % 2
        keep = lax.dynamic_index_in_dim(grouped, mine, 1, keepdims=False)
        send = lax.dynamic_index_in_dim(grouped, 1 - mine, 1, keepdims=False)
        received = lax.ppermute(send, axis_name, [(j, j ^ bit) for j in range(size)])
        held = (keep + received).reshape(blocks // 2 * rows, cols)
        bit *= 2
    return held


def solution(mesh):
    in_specs = (
        P(None, "pool"),
        P("pool", "tp"),
        P("tp", "pool"),
        P("pool", None, "tp"),
        P("pool", None, None, "tp"),
        P(),
        P(),
        P(),
        P(),
        P(),
    )
    out_specs = P("tp", "pool")
    return jax.shard_map(body, mesh=mesh, in_specs=in_specs, out_specs=out_specs, check_vma=False)
```

```python
import math

import jax
import jax.numpy as jnp
from jax import lax
from jax.sharding import PartitionSpec as P

H = 64
KVH = 8
HD = 128
DRAFT = 64
PAGE = 128
MAXP = 32
MAXRES = 8
USER_DEV = 2


ROPE_BASE = 500000.0


def ancestry_of(parents):
    users_count, draft_len = parents.shape
    tokens = jnp.arange(draft_len)
    reach = (parents[:, :, None] == tokens[None, None, :]).astype(jnp.float32)
    reach = reach + (tokens[:, None] == tokens[None, :]).astype(jnp.float32)[None]
    for unused in range(max(1, math.ceil(math.log2(draft_len)))):
        reach = jnp.minimum(
            jnp.einsum(
                "uij,ujk->uik",
                reach.astype(jnp.bfloat16),
                reach.astype(jnp.bfloat16),
                preferred_element_type=jnp.float32,
            ),
            1.0,
        )
    return reach


def rotate(vectors, positions):
    half_size = vectors.shape[-1] // 2
    frequencies = jnp.exp(
        jnp.arange(half_size).astype(jnp.float32) * (-2.0 * math.log(ROPE_BASE) / vectors.shape[-1])
    )
    angles = positions[..., None] * frequencies
    cosines = jnp.cos(angles)
    sines = jnp.sin(angles)
    lower_half = vectors[..., :half_size]
    upper_half = vectors[..., half_size:]
    return jnp.concatenate(
        [lower_half * cosines - upper_half * sines, upper_half * cosines + lower_half * sines], -1
    )


def attend_dense(queries, history, draft_key, draft_value, visible, length):
    heads_kv, row_count, head_dim = queries.shape
    score_scale = head_dim ** (-0.5)
    hist_ok = (jnp.arange(history.shape[0]) < length)[None, :]
    results = []
    for head in range(heads_kv):
        keys = history[:, 2 * head * head_dim : (2 * head + 1) * head_dim]
        values = history[:, (2 * head + 1) * head_dim : (2 * head + 2) * head_dim]
        hist_scores = (
            jnp.einsum("rd,sd->rs", queries[head], keys, preferred_element_type=jnp.float32)
            * score_scale
        )
        draft_scores = (
            jnp.einsum(
                "rd,jd->rj", queries[head], draft_key[:, head], preferred_element_type=jnp.float32
            )
            * score_scale
        )
        row_max = jnp.maximum(
            jnp.max(jnp.where(hist_ok, hist_scores, -jnp.inf), -1),
            jnp.max(jnp.where(visible, draft_scores, -jnp.inf), -1),
        )
        hist_weight = jnp.where(hist_ok, jnp.exp(hist_scores - row_max[:, None]), 0.0)
        draft_weight = jnp.where(visible, jnp.exp(draft_scores - row_max[:, None]), 0.0)
        denominator = jnp.sum(hist_weight, -1) + jnp.sum(draft_weight, -1)
        weighted = jnp.einsum(
            "rs,sd->rd",
            hist_weight.astype(jnp.bfloat16),
            values,
            preferred_element_type=jnp.float32,
        ) + jnp.einsum(
            "rj,jd->rd",
            draft_weight.astype(jnp.bfloat16),
            draft_value[:, head],
            preferred_element_type=jnp.float32,
        )
        results.append(weighted / denominator[:, None])
    return jnp.stack(results, 0)


def finish(result, draft_len):
    heads_kv, row_count, head_dim = result.shape
    result = result.reshape(heads_kv, draft_len, row_count // draft_len, head_dim).transpose(
        1, 0, 2, 3
    )
    return result.reshape(draft_len, heads_kv * row_count // draft_len * head_dim).astype(
        jnp.bfloat16
    )


def body(
    draft_states,
    w_qkv,
    w_out,
    kv_pool,
    resident_kv,
    page_owner,
    page_slot,
    hist_len,
    res_count,
    parents,
):
    pool_size = lax.axis_size("pool")
    my_index = lax.axis_index("pool")
    group_size = H // KVH
    local_cols = w_qkv.shape[1]
    heads_kv = local_cols // ((group_size + 2) * HD)
    projected = lax.psum_scatter(
        jnp.dot(draft_states, w_qkv, preferred_element_type=jnp.float32),
        "pool",
        scatter_dimension=0,
        tiled=True,
    )
    projected = projected.reshape(USER_DEV, DRAFT, heads_kv, group_size + 2, HD)
    first_user = my_index * USER_DEV
    my_lengths = lax.dynamic_slice_in_dim(hist_len, first_user, USER_DEV)
    my_resident = lax.dynamic_slice_in_dim(res_count, first_user, USER_DEV)
    my_parents = lax.dynamic_slice_in_dim(parents, first_user, USER_DEV, 0)
    ancestry = ancestry_of(my_parents)
    positions = my_lengths.astype(jnp.float32)[:, None] + jnp.sum(ancestry, -1) - 1.0
    queries = rotate(projected[:, :, :, :group_size], positions[:, :, None, None]).astype(
        jnp.bfloat16
    )
    draft_key = rotate(projected[:, :, :, group_size], positions[:, :, None]).astype(jnp.bfloat16)
    draft_value = projected[:, :, :, group_size + 1].astype(jnp.bfloat16)
    row_count = DRAFT * group_size
    query_rows = queries.transpose(0, 2, 1, 3, 4).reshape(USER_DEV, heads_kv, row_count, HD)
    visible = jnp.repeat(ancestry > 0.5, group_size, axis=1)
    block_rows = USER_DEV * MAXP
    capacity = block_rows // pool_size
    kv_cols = kv_pool.shape[2]
    owner_blocks = page_owner.reshape(pool_size, block_rows)
    slot_blocks = page_slot.reshape(pool_size, block_rows)
    one_hot = (owner_blocks[:, :, None] == jnp.arange(pool_size)[None, None, :]).astype(jnp.int32)
    slot_ranks = jnp.sum((jnp.cumsum(one_hot, axis=1) - one_hot) * one_hot, axis=2)
    hot_owner = jnp.argmax(jnp.sum(one_hot, axis=1), axis=1)
    mine = owner_blocks == my_index
    targets = jnp.arange(pool_size)[:, None] * capacity + slot_ranks
    send_to = jnp.where(mine & (slot_ranks < capacity), targets, pool_size * capacity)
    pack_index = (
        jnp.zeros((pool_size * capacity,), jnp.int32)
        .at[send_to.reshape(-1)]
        .set(slot_blocks.reshape(-1), mode="drop")
    )
    extra_to = jnp.where(mine & (slot_ranks >= capacity), slot_ranks - capacity, capacity)
    extra_index = (
        jnp.zeros((capacity,), jnp.int32)
        .at[extra_to.reshape(-1)]
        .set(slot_blocks.reshape(-1), mode="drop")
    )
    piece_rows = capacity * PAGE // pool_size
    arrived = lax.all_to_all(
        kv_pool[pack_index], "pool", split_axis=0, concat_axis=0, tiled=True
    )
    spread = lax.all_to_all(
        kv_pool[extra_index].reshape(pool_size, piece_rows, kv_cols),
        "pool",
        split_axis=0,
        concat_axis=0,
        tiled=True,
    )
    extra = lax.all_to_all(
        spread[hot_owner], "pool", split_axis=0, concat_axis=0, tiled=True
    ).reshape(capacity, PAGE, kv_cols)
    local_source = resident_kv.reshape(USER_DEV * MAXRES, PAGE, kv_cols)
    outputs = []
    my_owner = lax.dynamic_index_in_dim(owner_blocks, my_index, 0, keepdims=False).reshape(
        USER_DEV, MAXP
    )
    my_rank = lax.dynamic_index_in_dim(slot_ranks, my_index, 0, keepdims=False).reshape(
        USER_DEV, MAXP
    )
    numbers = jnp.arange(MAXP)
    for local_user in range(USER_DEV):
        owner = my_owner[local_user]
        rank = my_rank[local_user]
        resident_pages = local_source[local_user * MAXRES + jnp.minimum(numbers, MAXRES - 1)]
        regular_pages = arrived[owner * capacity + jnp.minimum(rank, capacity - 1)]
        extra_pages = extra[jnp.clip(rank - capacity, 0, capacity - 1)]
        history = jnp.where(
            (numbers < my_resident[local_user])[:, None, None],
            resident_pages,
            jnp.where((rank < capacity)[:, None, None], regular_pages, extra_pages),
        ).reshape(MAXP * PAGE, kv_cols)
        result = attend_dense(
            query_rows[local_user],
            history,
            draft_key[local_user],
            draft_value[local_user],
            visible[local_user],
            my_lengths[local_user],
        )
        outputs.append(finish(result, DRAFT))
    tp_size = lax.axis_size("tp")
    pieces = []
    for user_attention in outputs:
        partial_out = jnp.dot(
            lax.all_gather(user_attention, "pool", axis=0, tiled=True),
            w_out,
            preferred_element_type=jnp.float32,
        )
        pieces.append(halving_sum(partial_out, "tp").reshape(pool_size // tp_size, DRAFT, -1))
    return jnp.stack(pieces, 1).reshape(pool_size // tp_size * USER_DEV * DRAFT, -1).astype(
        jnp.bfloat16
    )


def halving_sum(partial, axis_name):
    size = lax.axis_size(axis_name)
    me = lax.axis_index(axis_name)
    rows = partial.shape[0] // size
    cols = partial.shape[1]
    held = partial
    bit = 1
    while bit < size:
        blocks = held.shape[0] // rows
        grouped = held.reshape(blocks // 2, 2, rows, cols)
        mine = (me // bit) % 2
        keep = lax.dynamic_index_in_dim(grouped, mine, 1, keepdims=False)
        send = lax.dynamic_index_in_dim(grouped, 1 - mine, 1, keepdims=False)
        received = lax.ppermute(send, axis_name, [(j, j ^ bit) for j in range(size)])
        held = (keep + received).reshape(blocks // 2 * rows, cols)
        bit *= 2
    return held


def solution(mesh):
    in_specs = (
        P(None, "pool"),
        P("pool", "tp"),
        P("tp", "pool"),
        P("pool", None, "tp"),
        P("pool", None, None, "tp"),
        P(),
        P(),
        P(),
        P(),
        P(),
    )
    out_specs = P("tp", "pool")
    return jax.shard_map(body, mesh=mesh, in_specs=in_specs, out_specs=out_specs, check_vma=False)
```

```python
import math

import jax
import jax.numpy as jnp
from jax import lax
from jax.sharding import PartitionSpec as P

H = 64
KVH = 8
HD = 128
DRAFT = 64
PAGE = 128
MAXP = 32
MAXRES = 8
USER_DEV = 2


ROPE_BASE = 500000.0


def ancestry_of(parents):
    users_count, draft_len = parents.shape
    tokens = jnp.arange(draft_len)
    reach = (parents[:, :, None] == tokens[None, None, :]).astype(jnp.float32)
    reach = reach + (tokens[:, None] == tokens[None, :]).astype(jnp.float32)[None]
    for unused in range(max(1, math.ceil(math.log2(draft_len)))):
        reach = jnp.minimum(
            jnp.einsum(
                "uij,ujk->uik",
                reach.astype(jnp.bfloat16),
                reach.astype(jnp.bfloat16),
                preferred_element_type=jnp.float32,
            ),
            1.0,
        )
    return reach


def rotate(vectors, positions):
    half_size = vectors.shape[-1] // 2
    frequencies = jnp.exp(
        jnp.arange(half_size).astype(jnp.float32) * (-2.0 * math.log(ROPE_BASE) / vectors.shape[-1])
    )
    angles = positions[..., None] * frequencies
    cosines = jnp.cos(angles)
    sines = jnp.sin(angles)
    lower_half = vectors[..., :half_size]
    upper_half = vectors[..., half_size:]
    return jnp.concatenate(
        [lower_half * cosines - upper_half * sines, upper_half * cosines + lower_half * sines], -1
    )


def attend_dense(queries, history, draft_key, draft_value, visible, length):
    heads_kv, row_count, head_dim = queries.shape
    score_scale = head_dim ** (-0.5)
    hist_ok = (jnp.arange(history.shape[0]) < length)[None, :]
    results = []
    for head in range(heads_kv):
        keys = history[:, 2 * head * head_dim : (2 * head + 1) * head_dim]
        values = history[:, (2 * head + 1) * head_dim : (2 * head + 2) * head_dim]
        hist_scores = (
            jnp.einsum("rd,sd->rs", queries[head], keys, preferred_element_type=jnp.float32)
            * score_scale
        )
        draft_scores = (
            jnp.einsum(
                "rd,jd->rj", queries[head], draft_key[:, head], preferred_element_type=jnp.float32
            )
            * score_scale
        )
        row_max = jnp.maximum(
            jnp.max(jnp.where(hist_ok, hist_scores, -jnp.inf), -1),
            jnp.max(jnp.where(visible, draft_scores, -jnp.inf), -1),
        )
        hist_weight = jnp.where(hist_ok, jnp.exp(hist_scores - row_max[:, None]), 0.0)
        draft_weight = jnp.where(visible, jnp.exp(draft_scores - row_max[:, None]), 0.0)
        denominator = jnp.sum(hist_weight, -1) + jnp.sum(draft_weight, -1)
        weighted = jnp.einsum(
            "rs,sd->rd",
            hist_weight.astype(jnp.bfloat16),
            values,
            preferred_element_type=jnp.float32,
        ) + jnp.einsum(
            "rj,jd->rd",
            draft_weight.astype(jnp.bfloat16),
            draft_value[:, head],
            preferred_element_type=jnp.float32,
        )
        results.append(weighted / denominator[:, None])
    return jnp.stack(results, 0)


def finish(result, draft_len):
    heads_kv, row_count, head_dim = result.shape
    result = result.reshape(heads_kv, draft_len, row_count // draft_len, head_dim).transpose(
        1, 0, 2, 3
    )
    return result.reshape(draft_len, heads_kv * row_count // draft_len * head_dim).astype(
        jnp.bfloat16
    )


def body(
    draft_states,
    w_qkv,
    w_out,
    kv_pool,
    resident_kv,
    page_owner,
    page_slot,
    hist_len,
    res_count,
    parents,
):
    pool_size = lax.axis_size("pool")
    my_index = lax.axis_index("pool")
    group_size = H // KVH
    local_cols = w_qkv.shape[1]
    heads_kv = local_cols // ((group_size + 2) * HD)
    projected = lax.psum_scatter(
        jnp.dot(draft_states, w_qkv, preferred_element_type=jnp.float32),
        "pool",
        scatter_dimension=0,
        tiled=True,
    )
    projected = projected.reshape(USER_DEV, DRAFT, heads_kv, group_size + 2, HD)
    first_user = my_index * USER_DEV
    my_lengths = lax.dynamic_slice_in_dim(hist_len, first_user, USER_DEV)
    my_resident = lax.dynamic_slice_in_dim(res_count, first_user, USER_DEV)
    my_parents = lax.dynamic_slice_in_dim(parents, first_user, USER_DEV, 0)
    ancestry = ancestry_of(my_parents)
    positions = my_lengths.astype(jnp.float32)[:, None] + jnp.sum(ancestry, -1) - 1.0
    queries = rotate(projected[:, :, :, :group_size], positions[:, :, None, None]).astype(
        jnp.bfloat16
    )
    draft_key = rotate(projected[:, :, :, group_size], positions[:, :, None]).astype(jnp.bfloat16)
    draft_value = projected[:, :, :, group_size + 1].astype(jnp.bfloat16)
    row_count = DRAFT * group_size
    query_rows = queries.transpose(0, 2, 1, 3, 4).reshape(USER_DEV, heads_kv, row_count, HD)
    visible = jnp.repeat(ancestry > 0.5, group_size, axis=1)
    block_rows = USER_DEV * MAXP
    capacity = block_rows // pool_size
    kv_cols = kv_pool.shape[2]
    owner_blocks = page_owner.reshape(pool_size, block_rows)
    slot_blocks = page_slot.reshape(pool_size, block_rows)
    one_hot = (owner_blocks[:, :, None] == jnp.arange(pool_size)[None, None, :]).astype(jnp.int32)
    slot_ranks = jnp.sum((jnp.cumsum(one_hot, axis=1) - one_hot) * one_hot, axis=2)
    hot_owner = jnp.argmax(jnp.sum(one_hot, axis=1), axis=1)
    mine = owner_blocks == my_index
    targets = jnp.arange(pool_size)[:, None] * capacity + slot_ranks
    send_to = jnp.where(mine & (slot_ranks < capacity), targets, pool_size * capacity)
    pack_index = (
        jnp.zeros((pool_size * capacity,), jnp.int32)
        .at[send_to.reshape(-1)]
        .set(slot_blocks.reshape(-1), mode="drop")
    )
    extra_to = jnp.where(mine & (slot_ranks >= capacity), slot_ranks - capacity, capacity)
    extra_index = (
        jnp.zeros((capacity,), jnp.int32)
        .at[extra_to.reshape(-1)]
        .set(slot_blocks.reshape(-1), mode="drop")
    )
    piece_rows = capacity * PAGE // pool_size
    arrived = lax.all_to_all(
        kv_pool[pack_index], "pool", split_axis=0, concat_axis=0, tiled=True
    )
    spread = lax.all_to_all(
        kv_pool[extra_index].reshape(pool_size, piece_rows, kv_cols),
        "pool",
        split_axis=0,
        concat_axis=0,
        tiled=True,
    )
    extra = lax.all_to_all(
        spread[hot_owner], "pool", split_axis=0, concat_axis=0, tiled=True
    ).reshape(capacity, PAGE, kv_cols)
    local_source = resident_kv.reshape(USER_DEV * MAXRES, PAGE, kv_cols)
    outputs = []
    my_owner = lax.dynamic_index_in_dim(owner_blocks, my_index, 0, keepdims=False).reshape(
        USER_DEV, MAXP
    )
    my_rank = lax.dynamic_index_in_dim(slot_ranks, my_index, 0, keepdims=False).reshape(
        USER_DEV, MAXP
    )
    numbers = jnp.arange(MAXP)
    for local_user in range(USER_DEV):
        owner = my_owner[local_user]
        rank = my_rank[local_user]
        resident_pages = local_source[local_user * MAXRES + jnp.minimum(numbers, MAXRES - 1)]
        regular_pages = arrived[owner * capacity + jnp.minimum(rank, capacity - 1)]
        extra_pages = extra[jnp.clip(rank - capacity, 0, capacity - 1)]
        history = jnp.where(
            (numbers < my_resident[local_user])[:, None, None],
            resident_pages,
            jnp.where((rank < capacity)[:, None, None], regular_pages, extra_pages),
        ).reshape(MAXP * PAGE, kv_cols)
        result = attend_dense(
            query_rows[local_user],
            history,
            draft_key[local_user],
            draft_value[local_user],
            visible[local_user],
            my_lengths[local_user],
        )
        outputs.append(finish(result, DRAFT))
    attention = jnp.concatenate(outputs, 0)
    partial_out = jnp.dot(
        lax.all_gather(attention, "pool", axis=0, tiled=True),
        w_out,
        preferred_element_type=jnp.float32,
    )
    return halving_sum(partial_out, "tp").astype(jnp.bfloat16)


def halving_sum(partial, axis_name):
    size = lax.axis_size(axis_name)
    me = lax.axis_index(axis_name)
    rows = partial.shape[0] // size
    cols = partial.shape[1]
    held = partial
    bit = 1
    while bit < size:
        blocks = held.shape[0] // rows
        grouped = held.reshape(blocks // 2, 2, rows, cols)
        mine = (me // bit) % 2
        keep = lax.dynamic_index_in_dim(grouped, mine, 1, keepdims=False)
        send = lax.dynamic_index_in_dim(grouped, 1 - mine, 1, keepdims=False)
        if bit > 1:
            send = send.astype(jnp.bfloat16)
        received = lax.ppermute(send, axis_name, [(j, j ^ bit) for j in range(size)])
        held = (keep + received.astype(jnp.float32)).reshape(blocks // 2 * rows, cols)
        bit *= 2
    return held


def solution(mesh):
    in_specs = (
        P(None, "pool"),
        P("pool", "tp"),
        P("tp", "pool"),
        P("pool", None, "tp"),
        P("pool", None, None, "tp"),
        P(),
        P(),
        P(),
        P(),
        P(),
    )
    out_specs = P("tp", "pool")
    return jax.shard_map(body, mesh=mesh, in_specs=in_specs, out_specs=out_specs, check_vma=False)
```

```python
import math

import jax
import jax.numpy as jnp
from jax import lax
from jax.sharding import PartitionSpec as P

H = 64
KVH = 8
HD = 128
DRAFT = 64
PAGE = 128
MAXP = 32
MAXRES = 8
USER_DEV = 2


ROPE_BASE = 500000.0


def ancestry_of(parents):
    users_count, draft_len = parents.shape
    tokens = jnp.arange(draft_len)
    reach = (parents[:, :, None] == tokens[None, None, :]).astype(jnp.float32)
    reach = reach + (tokens[:, None] == tokens[None, :]).astype(jnp.float32)[None]
    for unused in range(max(1, math.ceil(math.log2(draft_len)))):
        reach = jnp.minimum(
            jnp.einsum(
                "uij,ujk->uik",
                reach.astype(jnp.bfloat16),
                reach.astype(jnp.bfloat16),
                preferred_element_type=jnp.float32,
            ),
            1.0,
        )
    return reach


def rotate(vectors, positions):
    half_size = vectors.shape[-1] // 2
    frequencies = jnp.exp(
        jnp.arange(half_size).astype(jnp.float32) * (-2.0 * math.log(ROPE_BASE) / vectors.shape[-1])
    )
    angles = positions[..., None] * frequencies
    cosines = jnp.cos(angles)
    sines = jnp.sin(angles)
    lower_half = vectors[..., :half_size]
    upper_half = vectors[..., half_size:]
    return jnp.concatenate(
        [lower_half * cosines - upper_half * sines, upper_half * cosines + lower_half * sines], -1
    )


def attend_dense(queries, history, draft_key, draft_value, visible, length):
    heads_kv, row_count, head_dim = queries.shape
    score_scale = head_dim ** (-0.5)
    hist_ok = (jnp.arange(history.shape[0]) < length)[None, :]

    def attend_head(operands):
        head, head_queries, head_key, head_value = operands
        keys = lax.dynamic_slice_in_dim(history, 2 * head * head_dim, head_dim, axis=1)
        values = lax.dynamic_slice_in_dim(history, (2 * head + 1) * head_dim, head_dim, axis=1)
        hist_scores = (
            jnp.einsum("rd,sd->rs", head_queries, keys, preferred_element_type=jnp.float32)
            * score_scale
        )
        draft_scores = (
            jnp.einsum("rd,jd->rj", head_queries, head_key, preferred_element_type=jnp.float32)
            * score_scale
        )
        row_max = jnp.maximum(
            jnp.max(jnp.where(hist_ok, hist_scores, -jnp.inf), -1),
            jnp.max(jnp.where(visible, draft_scores, -jnp.inf), -1),
        )
        hist_weight = jnp.where(hist_ok, jnp.exp(hist_scores - row_max[:, None]), 0.0)
        draft_weight = jnp.where(visible, jnp.exp(draft_scores - row_max[:, None]), 0.0)
        denominator = jnp.sum(hist_weight, -1) + jnp.sum(draft_weight, -1)
        weighted = jnp.einsum(
            "rs,sd->rd",
            hist_weight.astype(jnp.bfloat16),
            values,
            preferred_element_type=jnp.float32,
        ) + jnp.einsum(
            "rj,jd->rd",
            draft_weight.astype(jnp.bfloat16),
            head_value,
            preferred_element_type=jnp.float32,
        )
        return weighted / denominator[:, None]

    return lax.map(
        attend_head,
        (
            jnp.arange(heads_kv),
            queries,
            draft_key.transpose(1, 0, 2),
            draft_value.transpose(1, 0, 2),
        ),
    )


def finish(result, draft_len):
    heads_kv, row_count, head_dim = result.shape
    result = result.reshape(heads_kv, draft_len, row_count // draft_len, head_dim).transpose(
        1, 0, 2, 3
    )
    return result.reshape(draft_len, heads_kv * row_count // draft_len * head_dim).astype(
        jnp.bfloat16
    )


def body(
    draft_states,
    w_qkv,
    w_out,
    kv_pool,
    resident_kv,
    page_owner,
    page_slot,
    hist_len,
    res_count,
    parents,
):
    pool_size = lax.axis_size("pool")
    my_index = lax.axis_index("pool")
    group_size = H // KVH
    local_cols = w_qkv.shape[1]
    heads_kv = local_cols // ((group_size + 2) * HD)
    projected = lax.psum_scatter(
        jnp.dot(draft_states, w_qkv, preferred_element_type=jnp.float32),
        "pool",
        scatter_dimension=0,
        tiled=True,
    )
    projected = projected.reshape(USER_DEV, DRAFT, heads_kv, group_size + 2, HD)
    first_user = my_index * USER_DEV
    my_lengths = lax.dynamic_slice_in_dim(hist_len, first_user, USER_DEV)
    my_resident = lax.dynamic_slice_in_dim(res_count, first_user, USER_DEV)
    my_parents = lax.dynamic_slice_in_dim(parents, first_user, USER_DEV, 0)
    ancestry = ancestry_of(my_parents)
    positions = my_lengths.astype(jnp.float32)[:, None] + jnp.sum(ancestry, -1) - 1.0
    queries = rotate(projected[:, :, :, :group_size], positions[:, :, None, None]).astype(
        jnp.bfloat16
    )
    draft_key = rotate(projected[:, :, :, group_size], positions[:, :, None]).astype(jnp.bfloat16)
    draft_value = projected[:, :, :, group_size + 1].astype(jnp.bfloat16)
    row_count = DRAFT * group_size
    query_rows = queries.transpose(0, 2, 1, 3, 4).reshape(USER_DEV, heads_kv, row_count, HD)
    visible = jnp.repeat(ancestry > 0.5, group_size, axis=1)
    block_rows = USER_DEV * MAXP
    capacity = block_rows // pool_size
    kv_cols = kv_pool.shape[2]
    owner_blocks = page_owner.reshape(pool_size, block_rows)
    slot_blocks = page_slot.reshape(pool_size, block_rows)
    one_hot = (owner_blocks[:, :, None] == jnp.arange(pool_size)[None, None, :]).astype(jnp.int32)
    slot_ranks = jnp.sum((jnp.cumsum(one_hot, axis=1) - one_hot) * one_hot, axis=2)
    hot_owner = jnp.argmax(jnp.sum(one_hot, axis=1), axis=1)
    mine = owner_blocks == my_index
    targets = jnp.arange(pool_size)[:, None] * capacity + slot_ranks
    send_to = jnp.where(mine & (slot_ranks < capacity), targets, pool_size * capacity)
    pack_index = (
        jnp.zeros((pool_size * capacity,), jnp.int32)
        .at[send_to.reshape(-1)]
        .set(slot_blocks.reshape(-1), mode="drop")
    )
    extra_to = jnp.where(mine & (slot_ranks >= capacity), slot_ranks - capacity, capacity)
    extra_index = (
        jnp.zeros((capacity,), jnp.int32)
        .at[extra_to.reshape(-1)]
        .set(slot_blocks.reshape(-1), mode="drop")
    )
    piece_rows = capacity * PAGE // pool_size
    arrived = lax.all_to_all(
        kv_pool[pack_index], "pool", split_axis=0, concat_axis=0, tiled=True
    )
    spread = lax.all_to_all(
        kv_pool[extra_index].reshape(pool_size, piece_rows, kv_cols),
        "pool",
        split_axis=0,
        concat_axis=0,
        tiled=True,
    )
    extra = lax.all_to_all(
        spread[hot_owner], "pool", split_axis=0, concat_axis=0, tiled=True
    ).reshape(capacity, PAGE, kv_cols)
    local_source = resident_kv.reshape(USER_DEV * MAXRES, PAGE, kv_cols)
    outputs = []
    my_owner = lax.dynamic_index_in_dim(owner_blocks, my_index, 0, keepdims=False).reshape(
        USER_DEV, MAXP
    )
    my_rank = lax.dynamic_index_in_dim(slot_ranks, my_index, 0, keepdims=False).reshape(
        USER_DEV, MAXP
    )
    numbers = jnp.arange(MAXP)
    for local_user in range(USER_DEV):
        owner = my_owner[local_user]
        rank = my_rank[local_user]
        resident_pages = local_source[local_user * MAXRES + jnp.minimum(numbers, MAXRES - 1)]
        regular_pages = arrived[owner * capacity + jnp.minimum(rank, capacity - 1)]
        extra_pages = extra[jnp.clip(rank - capacity, 0, capacity - 1)]
        history = jnp.where(
            (numbers < my_resident[local_user])[:, None, None],
            resident_pages,
            jnp.where((rank < capacity)[:, None, None], regular_pages, extra_pages),
        ).reshape(MAXP * PAGE, kv_cols)
        result = attend_dense(
            query_rows[local_user],
            history,
            draft_key[local_user],
            draft_value[local_user],
            visible[local_user],
            my_lengths[local_user],
        )
        outputs.append(finish(result, DRAFT))
    attention = jnp.concatenate(outputs, 0)
    partial_out = jnp.dot(
        lax.all_gather(attention, "pool", axis=0, tiled=True),
        w_out,
        preferred_element_type=jnp.float32,
    )
    return halving_sum(partial_out, "tp").astype(jnp.bfloat16)


def halving_sum(partial, axis_name):
    size = lax.axis_size(axis_name)
    me = lax.axis_index(axis_name)
    rows = partial.shape[0] // size
    cols = partial.shape[1]
    held = partial
    bit = 1
    while bit < size:
        blocks = held.shape[0] // rows
        grouped = held.reshape(blocks // 2, 2, rows, cols)
        mine = (me // bit) % 2
        keep = lax.dynamic_index_in_dim(grouped, mine, 1, keepdims=False)
        send = lax.dynamic_index_in_dim(grouped, 1 - mine, 1, keepdims=False)
        if bit > 1:
            send = send.astype(jnp.bfloat16)
        received = lax.ppermute(send, axis_name, [(j, j ^ bit) for j in range(size)])
        held = (keep + received.astype(jnp.float32)).reshape(blocks // 2 * rows, cols)
        bit *= 2
    return held


def solution(mesh):
    in_specs = (
        P(None, "pool"),
        P("pool", "tp"),
        P("tp", "pool"),
        P("pool", None, "tp"),
        P("pool", None, None, "tp"),
        P(),
        P(),
        P(),
        P(),
        P(),
    )
    out_specs = P("tp", "pool")
    return jax.shard_map(body, mesh=mesh, in_specs=in_specs, out_specs=out_specs, check_vma=False)
```

```python
import math

import jax
import jax.numpy as jnp
from jax import lax
from jax.sharding import PartitionSpec as P

H = 64
KVH = 8
HD = 128
DRAFT = 64
PAGE = 128
MAXP = 32
MAXRES = 8
USER_DEV = 2


ROPE_BASE = 500000.0


def ancestry_of(parents):
    users_count, draft_len = parents.shape
    tokens = jnp.arange(draft_len)
    reach = (parents[:, :, None] == tokens[None, None, :]).astype(jnp.float32)
    reach = reach + (tokens[:, None] == tokens[None, :]).astype(jnp.float32)[None]
    for unused in range(max(1, math.ceil(math.log2(draft_len)))):
        reach = jnp.minimum(
            jnp.einsum(
                "uij,ujk->uik",
                reach.astype(jnp.bfloat16),
                reach.astype(jnp.bfloat16),
                preferred_element_type=jnp.float32,
            ),
            1.0,
        )
    return reach


def rotate(vectors, positions):
    half_size = vectors.shape[-1] // 2
    frequencies = jnp.exp(
        jnp.arange(half_size).astype(jnp.float32) * (-2.0 * math.log(ROPE_BASE) / vectors.shape[-1])
    )
    angles = positions[..., None] * frequencies
    cosines = jnp.cos(angles)
    sines = jnp.sin(angles)
    lower_half = vectors[..., :half_size]
    upper_half = vectors[..., half_size:]
    return jnp.concatenate(
        [lower_half * cosines - upper_half * sines, upper_half * cosines + lower_half * sines], -1
    )


def attend_dense(queries, history, draft_key, draft_value, visible, length):
    heads_kv, row_count, head_dim = queries.shape
    score_scale = head_dim ** (-0.5)
    hist_ok = (jnp.arange(history.shape[0]) < length)[None, :]
    results = []
    for head in range(heads_kv):
        keys = history[:, 2 * head * head_dim : (2 * head + 1) * head_dim]
        values = history[:, (2 * head + 1) * head_dim : (2 * head + 2) * head_dim]
        hist_scores = (
            jnp.einsum("rd,sd->rs", queries[head], keys, preferred_element_type=jnp.float32)
            * score_scale
        )
        draft_scores = (
            jnp.einsum(
                "rd,jd->rj", queries[head], draft_key[:, head], preferred_element_type=jnp.float32
            )
            * score_scale
        )
        row_max = jnp.maximum(
            jnp.max(jnp.where(hist_ok, hist_scores, -jnp.inf), -1),
            jnp.max(jnp.where(visible, draft_scores, -jnp.inf), -1),
        )
        hist_weight = jnp.where(hist_ok, jnp.exp(hist_scores - row_max[:, None]), 0.0)
        draft_weight = jnp.where(visible, jnp.exp(draft_scores - row_max[:, None]), 0.0)
        denominator = jnp.sum(hist_weight, -1) + jnp.sum(draft_weight, -1)
        weighted = jnp.einsum(
            "rs,sd->rd",
            hist_weight.astype(jnp.bfloat16),
            values,
            preferred_element_type=jnp.float32,
        ) + jnp.einsum(
            "rj,jd->rd",
            draft_weight.astype(jnp.bfloat16),
            draft_value[:, head],
            preferred_element_type=jnp.float32,
        )
        results.append(weighted / denominator[:, None])
    return jnp.stack(results, 0)


def finish(result, draft_len):
    heads_kv, row_count, head_dim = result.shape
    result = result.reshape(heads_kv, draft_len, row_count // draft_len, head_dim).transpose(
        1, 0, 2, 3
    )
    return result.reshape(draft_len, heads_kv * row_count // draft_len * head_dim).astype(
        jnp.bfloat16
    )


def body(
    draft_states,
    w_qkv,
    w_out,
    kv_pool,
    resident_kv,
    page_owner,
    page_slot,
    hist_len,
    res_count,
    parents,
):
    pool_size = lax.axis_size("pool")
    my_index = lax.axis_index("pool")
    group_size = H // KVH
    local_cols = w_qkv.shape[1]
    heads_kv = local_cols // ((group_size + 2) * HD)
    projected = lax.psum_scatter(
        jnp.dot(draft_states, w_qkv, preferred_element_type=jnp.float32),
        "pool",
        scatter_dimension=0,
        tiled=True,
    )
    projected = projected.reshape(USER_DEV, DRAFT, heads_kv, group_size + 2, HD)
    first_user = my_index * USER_DEV
    my_lengths = lax.dynamic_slice_in_dim(hist_len, first_user, USER_DEV)
    my_resident = lax.dynamic_slice_in_dim(res_count, first_user, USER_DEV)
    my_parents = lax.dynamic_slice_in_dim(parents, first_user, USER_DEV, 0)
    ancestry = ancestry_of(my_parents)
    positions = my_lengths.astype(jnp.float32)[:, None] + jnp.sum(ancestry, -1) - 1.0
    queries = rotate(projected[:, :, :, :group_size], positions[:, :, None, None]).astype(
        jnp.bfloat16
    )
    draft_key = rotate(projected[:, :, :, group_size], positions[:, :, None]).astype(jnp.bfloat16)
    draft_value = projected[:, :, :, group_size + 1].astype(jnp.bfloat16)
    row_count = DRAFT * group_size
    query_rows = queries.transpose(0, 2, 1, 3, 4).reshape(USER_DEV, heads_kv, row_count, HD)
    visible = jnp.repeat(ancestry > 0.5, group_size, axis=1)
    block_rows = USER_DEV * MAXP
    capacity = block_rows // pool_size
    kv_cols = kv_pool.shape[2]
    owner_blocks = page_owner.reshape(pool_size, block_rows)
    slot_blocks = page_slot.reshape(pool_size, block_rows)
    one_hot = (owner_blocks[:, :, None] == jnp.arange(pool_size)[None, None, :]).astype(jnp.int32)
    slot_ranks = jnp.sum((jnp.cumsum(one_hot, axis=1) - one_hot) * one_hot, axis=2)
    hot_owner = jnp.argmax(jnp.sum(one_hot, axis=1), axis=1)
    mine = owner_blocks == my_index
    targets = jnp.arange(pool_size)[:, None] * capacity + slot_ranks
    send_to = jnp.where(mine & (slot_ranks < capacity), targets, pool_size * capacity)
    pack_index = (
        jnp.zeros((pool_size * capacity,), jnp.int32)
        .at[send_to.reshape(-1)]
        .set(slot_blocks.reshape(-1), mode="drop")
    )
    extra_to = jnp.where(mine & (slot_ranks >= capacity), slot_ranks - capacity, capacity)
    extra_index = (
        jnp.zeros((capacity,), jnp.int32)
        .at[extra_to.reshape(-1)]
        .set(slot_blocks.reshape(-1), mode="drop")
    )
    piece_rows = capacity * PAGE // pool_size
    arrived = lax.all_to_all(
        kv_pool[pack_index], "pool", split_axis=0, concat_axis=0, tiled=True
    )
    spread = lax.all_to_all(
        kv_pool[extra_index].reshape(pool_size, piece_rows, kv_cols),
        "pool",
        split_axis=0,
        concat_axis=0,
        tiled=True,
    )
    extra = lax.all_to_all(
        spread[hot_owner], "pool", split_axis=0, concat_axis=0, tiled=True
    ).reshape(capacity, PAGE, kv_cols)
    local_source = resident_kv.reshape(USER_DEV * MAXRES, PAGE, kv_cols)
    outputs = []
    my_owner = lax.dynamic_index_in_dim(owner_blocks, my_index, 0, keepdims=False).reshape(
        USER_DEV, MAXP
    )
    my_rank = lax.dynamic_index_in_dim(slot_ranks, my_index, 0, keepdims=False).reshape(
        USER_DEV, MAXP
    )
    numbers = jnp.arange(MAXP)
    for local_user in range(USER_DEV):
        owner = my_owner[local_user]
        rank = my_rank[local_user]
        resident_pages = local_source[local_user * MAXRES + jnp.minimum(numbers, MAXRES - 1)]
        regular_pages = arrived[owner * capacity + jnp.minimum(rank, capacity - 1)]
        extra_pages = extra[jnp.clip(rank - capacity, 0, capacity - 1)]
        history = jnp.where(
            (numbers < my_resident[local_user])[:, None, None],
            resident_pages,
            jnp.where((rank < capacity)[:, None, None], regular_pages, extra_pages),
        ).reshape(MAXP * PAGE, kv_cols)
        result = attend_dense(
            query_rows[local_user],
            history,
            draft_key[local_user],
            draft_value[local_user],
            visible[local_user],
            my_lengths[local_user],
        )
        outputs.append(finish(result, DRAFT))
    attention = jnp.concatenate(outputs, 0)
    gathered = lax.all_gather(attention, "pool", axis=0, tiled=True)
    half_cols = w_out.shape[1] // 2
    halves = [
        halving_sum(
            jnp.dot(
                gathered,
                w_out[:, part * half_cols : (part + 1) * half_cols],
                preferred_element_type=jnp.float32,
            ),
            "tp",
        )
        for part in range(2)
    ]
    return jnp.concatenate(halves, 1).astype(jnp.bfloat16)


def halving_sum(partial, axis_name):
    size = lax.axis_size(axis_name)
    me = lax.axis_index(axis_name)
    rows = partial.shape[0] // size
    cols = partial.shape[1]
    held = partial
    bit = 1
    while bit < size:
        blocks = held.shape[0] // rows
        grouped = held.reshape(blocks // 2, 2, rows, cols)
        mine = (me // bit) % 2
        keep = lax.dynamic_index_in_dim(grouped, mine, 1, keepdims=False)
        send = lax.dynamic_index_in_dim(grouped, 1 - mine, 1, keepdims=False)
        if bit > 1:
            send = send.astype(jnp.bfloat16)
        received = lax.ppermute(send, axis_name, [(j, j ^ bit) for j in range(size)])
        held = (keep + received.astype(jnp.float32)).reshape(blocks // 2 * rows, cols)
        bit *= 2
    return held


def solution(mesh):
    in_specs = (
        P(None, "pool"),
        P("pool", "tp"),
        P("tp", "pool"),
        P("pool", None, "tp"),
        P("pool", None, None, "tp"),
        P(),
        P(),
        P(),
        P(),
        P(),
    )
    out_specs = P("tp", "pool")
    return jax.shard_map(body, mesh=mesh, in_specs=in_specs, out_specs=out_specs, check_vma=False)
```

```python
import functools
import math

import jax
import jax.numpy as jnp
from jax import lax
from jax.sharding import PartitionSpec as P

H = 64
KVH = 8
HD = 128
DRAFT = 64
PAGE = 128
MAXP = 32
MAXRES = 8
USER_DEV = 2


ROPE_BASE = 500000.0


def ancestry_of(parents):
    users_count, draft_len = parents.shape
    tokens = jnp.arange(draft_len)
    reach = (parents[:, :, None] == tokens[None, None, :]).astype(jnp.float32)
    reach = reach + (tokens[:, None] == tokens[None, :]).astype(jnp.float32)[None]
    for unused in range(max(1, math.ceil(math.log2(draft_len)))):
        reach = jnp.minimum(
            jnp.einsum(
                "uij,ujk->uik",
                reach.astype(jnp.bfloat16),
                reach.astype(jnp.bfloat16),
                preferred_element_type=jnp.float32,
            ),
            1.0,
        )
    return reach


def rotate(vectors, positions):
    half_size = vectors.shape[-1] // 2
    frequencies = jnp.exp(
        jnp.arange(half_size).astype(jnp.float32) * (-2.0 * math.log(ROPE_BASE) / vectors.shape[-1])
    )
    angles = positions[..., None] * frequencies
    cosines = jnp.cos(angles)
    sines = jnp.sin(angles)
    lower_half = vectors[..., :half_size]
    upper_half = vectors[..., half_size:]
    return jnp.concatenate(
        [lower_half * cosines - upper_half * sines, upper_half * cosines + lower_half * sines], -1
    )


def attend_dense(queries, history, draft_key, draft_value, visible, length):
    heads_kv, row_count, head_dim = queries.shape
    score_scale = head_dim ** (-0.5)
    hist_ok = (jnp.arange(history.shape[0]) < length)[None, :]
    results = []
    for head in range(heads_kv):
        keys = history[:, 2 * head * head_dim : (2 * head + 1) * head_dim]
        values = history[:, (2 * head + 1) * head_dim : (2 * head + 2) * head_dim]
        hist_scores = (
            jnp.einsum("rd,sd->rs", queries[head], keys, preferred_element_type=jnp.float32)
            * score_scale
        )
        draft_scores = (
            jnp.einsum(
                "rd,jd->rj", queries[head], draft_key[:, head], preferred_element_type=jnp.float32
            )
            * score_scale
        )
        row_max = jnp.maximum(
            jnp.max(jnp.where(hist_ok, hist_scores, -jnp.inf), -1),
            jnp.max(jnp.where(visible, draft_scores, -jnp.inf), -1),
        )
        hist_weight = jnp.where(hist_ok, jnp.exp(hist_scores - row_max[:, None]), 0.0)
        draft_weight = jnp.where(visible, jnp.exp(draft_scores - row_max[:, None]), 0.0)
        denominator = jnp.sum(hist_weight, -1) + jnp.sum(draft_weight, -1)
        weighted = jnp.einsum(
            "rs,sd->rd",
            hist_weight.astype(jnp.bfloat16),
            values,
            preferred_element_type=jnp.float32,
        ) + jnp.einsum(
            "rj,jd->rd",
            draft_weight.astype(jnp.bfloat16),
            draft_value[:, head],
            preferred_element_type=jnp.float32,
        )
        results.append(weighted / denominator[:, None])
    return jnp.stack(results, 0)


def finish(result, draft_len):
    heads_kv, row_count, head_dim = result.shape
    result = result.reshape(heads_kv, draft_len, row_count // draft_len, head_dim).transpose(
        1, 0, 2, 3
    )
    return result.reshape(draft_len, heads_kv * row_count // draft_len * head_dim).astype(
        jnp.bfloat16
    )


def body(
    draft_states,
    w_qkv,
    w_out,
    kv_pool,
    resident_kv,
    page_owner,
    page_slot,
    hist_len,
    res_count,
    parents,
    ring,
):
    pool_size = lax.axis_size("pool")
    my_index = lax.axis_index("pool")
    group_size = H // KVH
    local_cols = w_qkv.shape[1]
    heads_kv = local_cols // ((group_size + 2) * HD)
    projected = lax.psum_scatter(
        jnp.dot(draft_states, w_qkv, preferred_element_type=jnp.float32),
        "pool",
        scatter_dimension=0,
        tiled=True,
    )
    projected = projected.reshape(USER_DEV, DRAFT, heads_kv, group_size + 2, HD)
    first_user = my_index * USER_DEV
    my_lengths = lax.dynamic_slice_in_dim(hist_len, first_user, USER_DEV)
    my_resident = lax.dynamic_slice_in_dim(res_count, first_user, USER_DEV)
    my_parents = lax.dynamic_slice_in_dim(parents, first_user, USER_DEV, 0)
    ancestry = ancestry_of(my_parents)
    positions = my_lengths.astype(jnp.float32)[:, None] + jnp.sum(ancestry, -1) - 1.0
    queries = rotate(projected[:, :, :, :group_size], positions[:, :, None, None]).astype(
        jnp.bfloat16
    )
    draft_key = rotate(projected[:, :, :, group_size], positions[:, :, None]).astype(jnp.bfloat16)
    draft_value = projected[:, :, :, group_size + 1].astype(jnp.bfloat16)
    row_count = DRAFT * group_size
    query_rows = queries.transpose(0, 2, 1, 3, 4).reshape(USER_DEV, heads_kv, row_count, HD)
    visible = jnp.repeat(ancestry > 0.5, group_size, axis=1)
    block_rows = USER_DEV * MAXP
    capacity = block_rows // pool_size
    kv_cols = kv_pool.shape[2]
    owner_blocks = page_owner.reshape(pool_size, block_rows)
    slot_blocks = page_slot.reshape(pool_size, block_rows)
    one_hot = (owner_blocks[:, :, None] == jnp.arange(pool_size)[None, None, :]).astype(jnp.int32)
    slot_ranks = jnp.sum((jnp.cumsum(one_hot, axis=1) - one_hot) * one_hot, axis=2)
    hot_owner = jnp.argmax(jnp.sum(one_hot, axis=1), axis=1)
    mine = owner_blocks == my_index
    targets = jnp.arange(pool_size)[:, None] * capacity + slot_ranks
    send_to = jnp.where(mine & (slot_ranks < capacity), targets, pool_size * capacity)
    pack_index = (
        jnp.zeros((pool_size * capacity,), jnp.int32)
        .at[send_to.reshape(-1)]
        .set(slot_blocks.reshape(-1), mode="drop")
    )
    extra_to = jnp.where(mine & (slot_ranks >= capacity), slot_ranks - capacity, capacity)
    extra_index = (
        jnp.zeros((capacity,), jnp.int32)
        .at[extra_to.reshape(-1)]
        .set(slot_blocks.reshape(-1), mode="drop")
    )
    piece_rows = capacity * PAGE // pool_size
    arrived = lax.all_to_all(
        kv_pool[pack_index], "pool", split_axis=0, concat_axis=0, tiled=True
    )
    spread = lax.all_to_all(
        kv_pool[extra_index].reshape(pool_size, piece_rows, kv_cols),
        "pool",
        split_axis=0,
        concat_axis=0,
        tiled=True,
    )
    extra = lax.all_to_all(
        spread[hot_owner], "pool", split_axis=0, concat_axis=0, tiled=True
    ).reshape(capacity, PAGE, kv_cols)
    local_source = resident_kv.reshape(USER_DEV * MAXRES, PAGE, kv_cols)
    outputs = []
    my_owner = lax.dynamic_index_in_dim(owner_blocks, my_index, 0, keepdims=False).reshape(
        USER_DEV, MAXP
    )
    my_rank = lax.dynamic_index_in_dim(slot_ranks, my_index, 0, keepdims=False).reshape(
        USER_DEV, MAXP
    )
    numbers = jnp.arange(MAXP)
    for local_user in range(USER_DEV):
        owner = my_owner[local_user]
        rank = my_rank[local_user]
        resident_pages = local_source[local_user * MAXRES + jnp.minimum(numbers, MAXRES - 1)]
        regular_pages = arrived[owner * capacity + jnp.minimum(rank, capacity - 1)]
        extra_pages = extra[jnp.clip(rank - capacity, 0, capacity - 1)]
        history = jnp.where(
            (numbers < my_resident[local_user])[:, None, None],
            resident_pages,
            jnp.where((rank < capacity)[:, None, None], regular_pages, extra_pages),
        ).reshape(MAXP * PAGE, kv_cols)
        result = attend_dense(
            query_rows[local_user],
            history,
            draft_key[local_user],
            draft_value[local_user],
            visible[local_user],
            my_lengths[local_user],
        )
        outputs.append(finish(result, DRAFT))
    attention = jnp.concatenate(outputs, 0)
    return halving_sum(ring_product(attention, w_out, "pool", ring), "tp").astype(jnp.bfloat16)


def ring_product(block, weights, axis_name, ring):
    count = len(ring)
    me = lax.axis_index(axis_name)
    ring_order = jnp.array(ring, jnp.int32)
    position = jnp.array([ring.index(index) for index in range(count)], jnp.int32)[me]
    forward = [(ring[k], ring[(k + 1) % count]) for k in range(count)]
    backward = [(ring[k], ring[(k - 1) % count]) for k in range(count)]
    product = jnp.zeros((count, block.shape[0], weights.shape[1]), jnp.float32)

    def place(product, rows, owner):
        return lax.dynamic_update_index_in_dim(
            product, jnp.dot(rows, weights, preferred_element_type=jnp.float32), owner, 0
        )

    product = place(product, block, me)
    ahead = block
    behind = block
    for step in range(1, count // 2 + 1):
        ahead = lax.ppermute(ahead, axis_name, forward)
        product = place(product, ahead, ring_order[(position - step) % count])
        if step < count - step:
            behind = lax.ppermute(behind, axis_name, backward)
            product = place(product, behind, ring_order[(position + step) % count])
    return product.reshape(count * block.shape[0], weights.shape[1])


def grid_ring(mesh):
    count = mesh.shape["pool"]
    try:
        places = {}
        for index in range(count):
            device = mesh.devices[index, 0]
            places[(device.coords[2], device.coords[0])] = index
        rows = sorted({z for z, x in places})
        cols = sorted({x for z, x in places})
        if len(rows) % 2 or len(rows) * len(cols) != count or len(cols) < 2:
            return list(range(count))
        cycle = [places[(z, cols[0])] for z in rows]
        for k, z in enumerate(reversed(rows)):
            line = cols[1:] if k % 2 == 0 else cols[:0:-1]
            cycle += [places[(z, x)] for x in line]
        return cycle
    except (AttributeError, IndexError, KeyError, TypeError):
        return list(range(count))


def halving_sum(partial, axis_name):
    size = lax.axis_size(axis_name)
    me = lax.axis_index(axis_name)
    rows = partial.shape[0] // size
    cols = partial.shape[1]
    held = partial
    bit = 1
    while bit < size:
        blocks = held.shape[0] // rows
        grouped = held.reshape(blocks // 2, 2, rows, cols)
        mine = (me // bit) % 2
        keep = lax.dynamic_index_in_dim(grouped, mine, 1, keepdims=False)
        send = lax.dynamic_index_in_dim(grouped, 1 - mine, 1, keepdims=False)
        if bit > 1:
            send = send.astype(jnp.bfloat16)
        received = lax.ppermute(send, axis_name, [(j, j ^ bit) for j in range(size)])
        held = (keep + received.astype(jnp.float32)).reshape(blocks // 2 * rows, cols)
        bit *= 2
    return held


def solution(mesh):
    in_specs = (
        P(None, "pool"),
        P("pool", "tp"),
        P("tp", "pool"),
        P("pool", None, "tp"),
        P("pool", None, None, "tp"),
        P(),
        P(),
        P(),
        P(),
        P(),
    )
    out_specs = P("tp", "pool")
    return jax.shard_map(functools.partial(body, ring=grid_ring(mesh)), mesh=mesh, in_specs=in_specs, out_specs=out_specs, check_vma=False)
```

```python
import functools
import math

import jax
import jax.numpy as jnp
from jax import lax
from jax.sharding import PartitionSpec as P

H = 64
KVH = 8
HD = 128
DRAFT = 64
PAGE = 128
MAXP = 32
MAXRES = 8
USER_DEV = 2


ROPE_BASE = 500000.0


def ancestry_of(parents):
    users_count, draft_len = parents.shape
    tokens = jnp.arange(draft_len)
    reach = (parents[:, :, None] == tokens[None, None, :]).astype(jnp.float32)
    reach = reach + (tokens[:, None] == tokens[None, :]).astype(jnp.float32)[None]
    for unused in range(max(1, math.ceil(math.log2(draft_len)))):
        reach = jnp.minimum(
            jnp.einsum(
                "uij,ujk->uik",
                reach.astype(jnp.bfloat16),
                reach.astype(jnp.bfloat16),
                preferred_element_type=jnp.float32,
            ),
            1.0,
        )
    return reach


def rotate(vectors, positions):
    half_size = vectors.shape[-1] // 2
    frequencies = jnp.exp(
        jnp.arange(half_size).astype(jnp.float32) * (-2.0 * math.log(ROPE_BASE) / vectors.shape[-1])
    )
    angles = positions[..., None] * frequencies
    cosines = jnp.cos(angles)
    sines = jnp.sin(angles)
    lower_half = vectors[..., :half_size]
    upper_half = vectors[..., half_size:]
    return jnp.concatenate(
        [lower_half * cosines - upper_half * sines, upper_half * cosines + lower_half * sines], -1
    )


def attend_dense(queries, history, draft_key, draft_value, visible, length):
    heads_kv, row_count, head_dim = queries.shape
    score_scale = head_dim ** (-0.5)
    hist_ok = (jnp.arange(history.shape[0]) < length)[None, :]
    results = []
    for head in range(heads_kv):
        keys = history[:, 2 * head * head_dim : (2 * head + 1) * head_dim]
        values = history[:, (2 * head + 1) * head_dim : (2 * head + 2) * head_dim]
        hist_scores = (
            jnp.einsum("rd,sd->rs", queries[head], keys, preferred_element_type=jnp.float32)
            * score_scale
        )
        draft_scores = (
            jnp.einsum(
                "rd,jd->rj", queries[head], draft_key[:, head], preferred_element_type=jnp.float32
            )
            * score_scale
        )
        row_max = jnp.maximum(
            jnp.max(jnp.where(hist_ok, hist_scores, -jnp.inf), -1),
            jnp.max(jnp.where(visible, draft_scores, -jnp.inf), -1),
        )
        hist_weight = jnp.where(hist_ok, jnp.exp(hist_scores - row_max[:, None]), 0.0)
        draft_weight = jnp.where(visible, jnp.exp(draft_scores - row_max[:, None]), 0.0)
        denominator = jnp.sum(hist_weight, -1) + jnp.sum(draft_weight, -1)
        weighted = jnp.einsum(
            "rs,sd->rd",
            hist_weight.astype(jnp.bfloat16),
            values,
            preferred_element_type=jnp.float32,
        ) + jnp.einsum(
            "rj,jd->rd",
            draft_weight.astype(jnp.bfloat16),
            draft_value[:, head],
            preferred_element_type=jnp.float32,
        )
        results.append(weighted / denominator[:, None])
    return jnp.stack(results, 0)


def finish(result, draft_len):
    heads_kv, row_count, head_dim = result.shape
    result = result.reshape(heads_kv, draft_len, row_count // draft_len, head_dim).transpose(
        1, 0, 2, 3
    )
    return result.reshape(draft_len, heads_kv * row_count // draft_len * head_dim).astype(
        jnp.bfloat16
    )


def body(
    draft_states,
    w_qkv,
    w_out,
    kv_pool,
    resident_kv,
    page_owner,
    page_slot,
    hist_len,
    res_count,
    parents,
    ring,
):
    pool_size = lax.axis_size("pool")
    my_index = lax.axis_index("pool")
    group_size = H // KVH
    local_cols = w_qkv.shape[1]
    heads_kv = local_cols // ((group_size + 2) * HD)
    projected = lax.psum_scatter(
        jnp.dot(draft_states, w_qkv, preferred_element_type=jnp.float32),
        "pool",
        scatter_dimension=0,
        tiled=True,
    )
    projected = projected.reshape(USER_DEV, DRAFT, heads_kv, group_size + 2, HD)
    first_user = my_index * USER_DEV
    my_lengths = lax.dynamic_slice_in_dim(hist_len, first_user, USER_DEV)
    my_resident = lax.dynamic_slice_in_dim(res_count, first_user, USER_DEV)
    my_parents = lax.dynamic_slice_in_dim(parents, first_user, USER_DEV, 0)
    ancestry = ancestry_of(my_parents)
    positions = my_lengths.astype(jnp.float32)[:, None] + jnp.sum(ancestry, -1) - 1.0
    queries = rotate(projected[:, :, :, :group_size], positions[:, :, None, None]).astype(
        jnp.bfloat16
    )
    draft_key = rotate(projected[:, :, :, group_size], positions[:, :, None]).astype(jnp.bfloat16)
    draft_value = projected[:, :, :, group_size + 1].astype(jnp.bfloat16)
    row_count = DRAFT * group_size
    query_rows = queries.transpose(0, 2, 1, 3, 4).reshape(USER_DEV, heads_kv, row_count, HD)
    visible = jnp.repeat(ancestry > 0.5, group_size, axis=1)
    block_rows = USER_DEV * MAXP
    capacity = block_rows // pool_size
    kv_cols = kv_pool.shape[2]
    owner_blocks = page_owner.reshape(pool_size, block_rows)
    slot_blocks = page_slot.reshape(pool_size, block_rows)
    one_hot = (owner_blocks[:, :, None] == jnp.arange(pool_size)[None, None, :]).astype(jnp.int32)
    slot_ranks = jnp.sum((jnp.cumsum(one_hot, axis=1) - one_hot) * one_hot, axis=2)
    hot_owner = jnp.argmax(jnp.sum(one_hot, axis=1), axis=1)
    mine = owner_blocks == my_index
    targets = jnp.arange(pool_size)[:, None] * capacity + slot_ranks
    send_to = jnp.where(mine & (slot_ranks < capacity), targets, pool_size * capacity)
    pack_index = (
        jnp.zeros((pool_size * capacity,), jnp.int32)
        .at[send_to.reshape(-1)]
        .set(slot_blocks.reshape(-1), mode="drop")
    )
    extra_to = jnp.where(mine & (slot_ranks >= capacity), slot_ranks - capacity, capacity)
    extra_index = (
        jnp.zeros((capacity,), jnp.int32)
        .at[extra_to.reshape(-1)]
        .set(slot_blocks.reshape(-1), mode="drop")
    )
    piece_rows = capacity * PAGE // pool_size
    arrived = lax.all_to_all(
        kv_pool[pack_index], "pool", split_axis=0, concat_axis=0, tiled=True
    )
    spread = lax.all_to_all(
        kv_pool[extra_index].reshape(pool_size, piece_rows, kv_cols),
        "pool",
        split_axis=0,
        concat_axis=0,
        tiled=True,
    )
    extra = lax.all_to_all(
        spread[hot_owner], "pool", split_axis=0, concat_axis=0, tiled=True
    ).reshape(capacity, PAGE, kv_cols)
    local_source = resident_kv.reshape(USER_DEV * MAXRES, PAGE, kv_cols)
    outputs = []
    my_owner = lax.dynamic_index_in_dim(owner_blocks, my_index, 0, keepdims=False).reshape(
        USER_DEV, MAXP
    )
    my_rank = lax.dynamic_index_in_dim(slot_ranks, my_index, 0, keepdims=False).reshape(
        USER_DEV, MAXP
    )
    numbers = jnp.arange(MAXP)
    for local_user in range(USER_DEV):
        owner = my_owner[local_user]
        rank = my_rank[local_user]
        resident_pages = local_source[local_user * MAXRES + jnp.minimum(numbers, MAXRES - 1)]
        regular_pages = arrived[owner * capacity + jnp.minimum(rank, capacity - 1)]
        extra_pages = extra[jnp.clip(rank - capacity, 0, capacity - 1)]
        history = jnp.where(
            (numbers < my_resident[local_user])[:, None, None],
            resident_pages,
            jnp.where((rank < capacity)[:, None, None], regular_pages, extra_pages),
        ).reshape(MAXP * PAGE, kv_cols)
        result = attend_dense(
            query_rows[local_user],
            history,
            draft_key[local_user],
            draft_value[local_user],
            visible[local_user],
            my_lengths[local_user],
        )
        outputs.append(finish(result, DRAFT))
    attention = jnp.concatenate(outputs, 0)
    return halving_sum(ring_product(attention, w_out, "pool", ring), "tp").astype(jnp.bfloat16)


def ring_product(block, weights, axis_name, ring):
    count = len(ring)
    me = lax.axis_index(axis_name)
    ring_order = jnp.array(ring, jnp.int32)
    position = jnp.array([ring.index(index) for index in range(count)], jnp.int32)[me]
    forward = [(ring[k], ring[(k + 1) % count]) for k in range(count)]
    backward = [(ring[k], ring[(k - 1) % count]) for k in range(count)]
    product = jnp.zeros((count, block.shape[0], weights.shape[1]), jnp.float32)

    def place(product, rows, owner):
        return lax.dynamic_update_index_in_dim(
            product, jnp.dot(rows, weights, preferred_element_type=jnp.float32), owner, 0
        )

    product = place(product, block, me)
    ahead = block
    behind = block
    half = block.shape[0] // 2
    for step in range(1, count // 2 + 1):
        if step < count - step:
            ahead = lax.ppermute(ahead, axis_name, forward)
            product = place(product, ahead, ring_order[(position - step) % count])
            behind = lax.ppermute(behind, axis_name, backward)
            product = place(product, behind, ring_order[(position + step) % count])
        else:
            first = lax.ppermute(ahead[:half], axis_name, forward)
            second = lax.ppermute(behind[half:], axis_name, backward)
            product = place(
                product, jnp.concatenate([first, second], 0), ring_order[(position - step) % count]
            )
    return product.reshape(count * block.shape[0], weights.shape[1])


def grid_ring(mesh):
    count = mesh.shape["pool"]
    try:
        places = {}
        for index in range(count):
            device = mesh.devices[index, 0]
            places[(device.coords[2], device.coords[0])] = index
        rows = sorted({z for z, x in places})
        cols = sorted({x for z, x in places})
        if len(rows) % 2 or len(rows) * len(cols) != count or len(cols) < 2:
            return list(range(count))
        cycle = [places[(z, cols[0])] for z in rows]
        for k, z in enumerate(reversed(rows)):
            line = cols[1:] if k % 2 == 0 else cols[:0:-1]
            cycle += [places[(z, x)] for x in line]
        return cycle
    except (AttributeError, IndexError, KeyError, TypeError):
        return list(range(count))


def halving_sum(partial, axis_name):
    size = lax.axis_size(axis_name)
    me = lax.axis_index(axis_name)
    rows = partial.shape[0] // size
    cols = partial.shape[1]
    held = partial
    bit = 1
    while bit < size:
        blocks = held.shape[0] // rows
        grouped = held.reshape(blocks // 2, 2, rows, cols)
        mine = (me // bit) % 2
        keep = lax.dynamic_index_in_dim(grouped, mine, 1, keepdims=False)
        send = lax.dynamic_index_in_dim(grouped, 1 - mine, 1, keepdims=False)
        if bit > 1:
            send = send.astype(jnp.bfloat16)
        received = lax.ppermute(send, axis_name, [(j, j ^ bit) for j in range(size)])
        held = (keep + received.astype(jnp.float32)).reshape(blocks // 2 * rows, cols)
        bit *= 2
    return held


def solution(mesh):
    in_specs = (
        P(None, "pool"),
        P("pool", "tp"),
        P("tp", "pool"),
        P("pool", None, "tp"),
        P("pool", None, None, "tp"),
        P(),
        P(),
        P(),
        P(),
        P(),
    )
    out_specs = P("tp", "pool")
    return jax.shard_map(functools.partial(body, ring=grid_ring(mesh)), mesh=mesh, in_specs=in_specs, out_specs=out_specs, check_vma=False)
```

```python
import functools
import math

import jax
import jax.numpy as jnp
from jax import lax
from jax.sharding import PartitionSpec as P

H = 64
KVH = 8
HD = 128
DRAFT = 64
PAGE = 128
MAXP = 32
MAXRES = 8
USER_DEV = 2


ROPE_BASE = 500000.0


def ancestry_of(parents):
    users_count, draft_len = parents.shape
    tokens = jnp.arange(draft_len)
    reach = (parents[:, :, None] == tokens[None, None, :]).astype(jnp.float32)
    reach = reach + (tokens[:, None] == tokens[None, :]).astype(jnp.float32)[None]
    for unused in range(max(1, math.ceil(math.log2(draft_len)))):
        reach = jnp.minimum(
            jnp.einsum(
                "uij,ujk->uik",
                reach.astype(jnp.bfloat16),
                reach.astype(jnp.bfloat16),
                preferred_element_type=jnp.float32,
            ),
            1.0,
        )
    return reach


def rotate(vectors, positions):
    half_size = vectors.shape[-1] // 2
    frequencies = jnp.exp(
        jnp.arange(half_size).astype(jnp.float32) * (-2.0 * math.log(ROPE_BASE) / vectors.shape[-1])
    )
    angles = positions[..., None] * frequencies
    cosines = jnp.cos(angles)
    sines = jnp.sin(angles)
    lower_half = vectors[..., :half_size]
    upper_half = vectors[..., half_size:]
    return jnp.concatenate(
        [lower_half * cosines - upper_half * sines, upper_half * cosines + lower_half * sines], -1
    )


def attend_dense(queries, history, draft_key, draft_value, visible, length):
    heads_kv, row_count, head_dim = queries.shape
    score_scale = head_dim ** (-0.5)
    hist_ok = (jnp.arange(history.shape[0]) < length)[None, :]
    results = []
    for head in range(heads_kv):
        keys = history[:, 2 * head * head_dim : (2 * head + 1) * head_dim]
        values = history[:, (2 * head + 1) * head_dim : (2 * head + 2) * head_dim]
        hist_scores = (
            jnp.einsum("rd,sd->rs", queries[head], keys, preferred_element_type=jnp.float32)
            * score_scale
        )
        draft_scores = (
            jnp.einsum(
                "rd,jd->rj", queries[head], draft_key[:, head], preferred_element_type=jnp.float32
            )
            * score_scale
        )
        row_max = jnp.maximum(
            jnp.max(jnp.where(hist_ok, hist_scores, -jnp.inf), -1),
            jnp.max(jnp.where(visible, draft_scores, -jnp.inf), -1),
        )
        hist_weight = jnp.where(hist_ok, jnp.exp(hist_scores - row_max[:, None]), 0.0)
        draft_weight = jnp.where(visible, jnp.exp(draft_scores - row_max[:, None]), 0.0)
        denominator = jnp.sum(hist_weight, -1) + jnp.sum(draft_weight, -1)
        weighted = jnp.einsum(
            "rs,sd->rd",
            hist_weight.astype(jnp.bfloat16),
            values,
            preferred_element_type=jnp.float32,
        ) + jnp.einsum(
            "rj,jd->rd",
            draft_weight.astype(jnp.bfloat16),
            draft_value[:, head],
            preferred_element_type=jnp.float32,
        )
        results.append(weighted / denominator[:, None])
    return jnp.stack(results, 0)


def finish(result, draft_len):
    heads_kv, row_count, head_dim = result.shape
    result = result.reshape(heads_kv, draft_len, row_count // draft_len, head_dim).transpose(
        1, 0, 2, 3
    )
    return result.reshape(draft_len, heads_kv * row_count // draft_len * head_dim).astype(
        jnp.bfloat16
    )


def body(
    draft_states,
    w_qkv,
    w_out,
    kv_pool,
    resident_kv,
    page_owner,
    page_slot,
    hist_len,
    res_count,
    parents,
    ring,
):
    pool_size = lax.axis_size("pool")
    my_index = lax.axis_index("pool")
    group_size = H // KVH
    local_cols = w_qkv.shape[1]
    heads_kv = local_cols // ((group_size + 2) * HD)
    projected = lax.psum_scatter(
        jnp.dot(draft_states, w_qkv, preferred_element_type=jnp.float32),
        "pool",
        scatter_dimension=0,
        tiled=True,
    )
    projected = projected.reshape(USER_DEV, DRAFT, heads_kv, group_size + 2, HD)
    first_user = my_index * USER_DEV
    my_lengths = lax.dynamic_slice_in_dim(hist_len, first_user, USER_DEV)
    my_resident = lax.dynamic_slice_in_dim(res_count, first_user, USER_DEV)
    my_parents = lax.dynamic_slice_in_dim(parents, first_user, USER_DEV, 0)
    ancestry = ancestry_of(my_parents)
    positions = my_lengths.astype(jnp.float32)[:, None] + jnp.sum(ancestry, -1) - 1.0
    queries = rotate(projected[:, :, :, :group_size], positions[:, :, None, None]).astype(
        jnp.bfloat16
    )
    draft_key = rotate(projected[:, :, :, group_size], positions[:, :, None]).astype(jnp.bfloat16)
    draft_value = projected[:, :, :, group_size + 1].astype(jnp.bfloat16)
    row_count = DRAFT * group_size
    query_rows = queries.transpose(0, 2, 1, 3, 4).reshape(USER_DEV, heads_kv, row_count, HD)
    visible = jnp.repeat(ancestry > 0.5, group_size, axis=1)
    block_rows = USER_DEV * MAXP
    capacity = block_rows // pool_size
    kv_cols = kv_pool.shape[2]
    owner_blocks = page_owner.reshape(pool_size, block_rows)
    slot_blocks = page_slot.reshape(pool_size, block_rows)
    one_hot = (owner_blocks[:, :, None] == jnp.arange(pool_size)[None, None, :]).astype(jnp.int32)
    slot_ranks = jnp.sum((jnp.cumsum(one_hot, axis=1) - one_hot) * one_hot, axis=2)
    hot_owner = jnp.argmax(jnp.sum(one_hot, axis=1), axis=1)
    mine = owner_blocks == my_index
    targets = jnp.arange(pool_size)[:, None] * capacity + slot_ranks
    send_to = jnp.where(mine & (slot_ranks < capacity), targets, pool_size * capacity)
    pack_index = (
        jnp.zeros((pool_size * capacity,), jnp.int32)
        .at[send_to.reshape(-1)]
        .set(slot_blocks.reshape(-1), mode="drop")
    )
    extra_to = jnp.where(mine & (slot_ranks >= capacity), slot_ranks - capacity, capacity)
    extra_index = (
        jnp.zeros((capacity,), jnp.int32)
        .at[extra_to.reshape(-1)]
        .set(slot_blocks.reshape(-1), mode="drop")
    )
    piece_rows = capacity * PAGE // pool_size
    arrived = lax.all_to_all(
        kv_pool[pack_index], "pool", split_axis=0, concat_axis=0, tiled=True
    )
    spread = lax.all_to_all(
        kv_pool[extra_index].reshape(pool_size, piece_rows, kv_cols),
        "pool",
        split_axis=0,
        concat_axis=0,
        tiled=True,
    )
    extra = lax.all_to_all(
        spread[hot_owner], "pool", split_axis=0, concat_axis=0, tiled=True
    ).reshape(capacity, PAGE, kv_cols)
    local_source = resident_kv.reshape(USER_DEV * MAXRES, PAGE, kv_cols)
    outputs = []
    my_owner = lax.dynamic_index_in_dim(owner_blocks, my_index, 0, keepdims=False).reshape(
        USER_DEV, MAXP
    )
    my_rank = lax.dynamic_index_in_dim(slot_ranks, my_index, 0, keepdims=False).reshape(
        USER_DEV, MAXP
    )
    numbers = jnp.arange(MAXP)
    for local_user in range(USER_DEV):
        owner = my_owner[local_user]
        rank = my_rank[local_user]
        resident_pages = local_source[local_user * MAXRES + jnp.minimum(numbers, MAXRES - 1)]
        regular_pages = arrived[owner * capacity + jnp.minimum(rank, capacity - 1)]
        extra_pages = extra[jnp.clip(rank - capacity, 0, capacity - 1)]
        history = jnp.where(
            (numbers < my_resident[local_user])[:, None, None],
            resident_pages,
            jnp.where((rank < capacity)[:, None, None], regular_pages, extra_pages),
        ).reshape(MAXP * PAGE, kv_cols)
        result = attend_dense(
            query_rows[local_user],
            history,
            draft_key[local_user],
            draft_value[local_user],
            visible[local_user],
            my_lengths[local_user],
        )
        outputs.append(finish(result, DRAFT))
    attention = jnp.concatenate(outputs, 0)
    return halving_sum(ring_product(attention, w_out, "pool", ring), "tp", 2).astype(jnp.bfloat16)


def ring_product(block, weights, axis_name, ring):
    count = len(ring)
    me = lax.axis_index(axis_name)
    tp_size = lax.axis_size("tp")
    tp_bit = lax.axis_index("tp") % 2
    ring_order = jnp.array(ring, jnp.int32)
    position = jnp.array([ring.index(index) for index in range(count)], jnp.int32)[me]
    forward = [(ring[k], ring[(k + 1) % count]) for k in range(count)]
    backward = [(ring[k], ring[(k - 1) % count]) for k in range(count)]
    block_rows = block.shape[0]
    cols = weights.shape[1]
    per_tp = count * block_rows // tp_size // block_rows
    slots = jnp.zeros((tp_size // 2 + 1, per_tp, block_rows, cols), jnp.float32)
    pairs = [(j, j ^ 1) for j in range(tp_size)]

    def place(slots, rows, owner):
        product = jnp.dot(rows, weights, preferred_element_type=jnp.float32)
        total = product + lax.ppermute(product, "tp", pairs)
        target = owner // per_tp
        slot = jnp.where(target % 2 == tp_bit, target // 2, tp_size // 2)
        return lax.dynamic_update_slice(slots, total[None, None], (slot, owner % per_tp, 0, 0))

    slots = place(slots, block, me)
    ahead = block
    behind = block
    half = block_rows // 2
    for step in range(1, count // 2 + 1):
        if step < count - step:
            ahead = lax.ppermute(ahead, axis_name, forward)
            slots = place(slots, ahead, ring_order[(position - step) % count])
            behind = lax.ppermute(behind, axis_name, backward)
            slots = place(slots, behind, ring_order[(position + step) % count])
        else:
            first = lax.ppermute(ahead[:half], axis_name, forward)
            second = lax.ppermute(behind[half:], axis_name, backward)
            slots = place(
                slots, jnp.concatenate([first, second], 0), ring_order[(position - step) % count]
            )
    return slots[: tp_size // 2].reshape(tp_size // 2 * per_tp * block_rows, cols)


def grid_ring(mesh):
    count = mesh.shape["pool"]
    try:
        places = {}
        for index in range(count):
            device = mesh.devices[index, 0]
            places[(device.coords[2], device.coords[0])] = index
        rows = sorted({z for z, x in places})
        cols = sorted({x for z, x in places})
        if len(rows) % 2 or len(rows) * len(cols) != count or len(cols) < 2:
            return list(range(count))
        cycle = [places[(z, cols[0])] for z in rows]
        for k, z in enumerate(reversed(rows)):
            line = cols[1:] if k % 2 == 0 else cols[:0:-1]
            cycle += [places[(z, x)] for x in line]
        return cycle
    except (AttributeError, IndexError, KeyError, TypeError):
        return list(range(count))


def halving_sum(partial, axis_name, bit):
    size = lax.axis_size(axis_name)
    me = lax.axis_index(axis_name)
    rows = partial.shape[0] * bit // size
    cols = partial.shape[1]
    held = partial
    while bit < size:
        blocks = held.shape[0] // rows
        grouped = held.reshape(blocks // 2, 2, rows, cols)
        mine = (me // bit) % 2
        keep = lax.dynamic_index_in_dim(grouped, mine, 1, keepdims=False)
        send = lax.dynamic_index_in_dim(grouped, 1 - mine, 1, keepdims=False)
        if bit > 1:
            send = send.astype(jnp.bfloat16)
        received = lax.ppermute(send, axis_name, [(j, j ^ bit) for j in range(size)])
        held = (keep + received.astype(jnp.float32)).reshape(blocks // 2 * rows, cols)
        bit *= 2
    return held


def solution(mesh):
    in_specs = (
        P(None, "pool"),
        P("pool", "tp"),
        P("tp", "pool"),
        P("pool", None, "tp"),
        P("pool", None, None, "tp"),
        P(),
        P(),
        P(),
        P(),
        P(),
    )
    out_specs = P("tp", "pool")
    return jax.shard_map(functools.partial(body, ring=grid_ring(mesh)), mesh=mesh, in_specs=in_specs, out_specs=out_specs, check_vma=False)
```

```python
import functools
import math

import jax
import jax.numpy as jnp
from jax import lax
from jax.sharding import PartitionSpec as P

H = 64
KVH = 8
HD = 128
DRAFT = 64
PAGE = 128
MAXP = 32
MAXRES = 8
USER_DEV = 2


ROPE_BASE = 500000.0


def ancestry_of(parents):
    users_count, draft_len = parents.shape
    tokens = jnp.arange(draft_len)
    reach = (parents[:, :, None] == tokens[None, None, :]).astype(jnp.float32)
    reach = reach + (tokens[:, None] == tokens[None, :]).astype(jnp.float32)[None]
    for unused in range(max(1, math.ceil(math.log2(draft_len)))):
        reach = jnp.minimum(
            jnp.einsum(
                "uij,ujk->uik",
                reach.astype(jnp.bfloat16),
                reach.astype(jnp.bfloat16),
                preferred_element_type=jnp.float32,
            ),
            1.0,
        )
    return reach


def rotate(vectors, positions):
    half_size = vectors.shape[-1] // 2
    frequencies = jnp.exp(
        jnp.arange(half_size).astype(jnp.float32) * (-2.0 * math.log(ROPE_BASE) / vectors.shape[-1])
    )
    angles = positions[..., None] * frequencies
    cosines = jnp.cos(angles)
    sines = jnp.sin(angles)
    lower_half = vectors[..., :half_size]
    upper_half = vectors[..., half_size:]
    return jnp.concatenate(
        [lower_half * cosines - upper_half * sines, upper_half * cosines + lower_half * sines], -1
    )


def attend_dense(queries, history, draft_key, draft_value, visible, length):
    heads_kv, row_count, head_dim = queries.shape
    score_scale = head_dim ** (-0.5)
    hist_ok = (jnp.arange(history.shape[0]) < length)[None, :]
    results = []
    for head in range(heads_kv):
        keys = history[:, 2 * head * head_dim : (2 * head + 1) * head_dim]
        values = history[:, (2 * head + 1) * head_dim : (2 * head + 2) * head_dim]
        hist_scores = (
            jnp.einsum("rd,sd->rs", queries[head], keys, preferred_element_type=jnp.float32)
            * score_scale
        )
        draft_scores = (
            jnp.einsum(
                "rd,jd->rj", queries[head], draft_key[:, head], preferred_element_type=jnp.float32
            )
            * score_scale
        )
        row_max = jnp.maximum(
            jnp.max(jnp.where(hist_ok, hist_scores, -jnp.inf), -1),
            jnp.max(jnp.where(visible, draft_scores, -jnp.inf), -1),
        )
        hist_weight = jnp.where(hist_ok, jnp.exp(hist_scores - row_max[:, None]), 0.0)
        draft_weight = jnp.where(visible, jnp.exp(draft_scores - row_max[:, None]), 0.0)
        denominator = jnp.sum(hist_weight, -1) + jnp.sum(draft_weight, -1)
        weighted = jnp.einsum(
            "rs,sd->rd",
            hist_weight.astype(jnp.bfloat16),
            values,
            preferred_element_type=jnp.float32,
        ) + jnp.einsum(
            "rj,jd->rd",
            draft_weight.astype(jnp.bfloat16),
            draft_value[:, head],
            preferred_element_type=jnp.float32,
        )
        results.append(weighted / denominator[:, None])
    return jnp.stack(results, 0)


def finish(result, draft_len):
    heads_kv, row_count, head_dim = result.shape
    result = result.reshape(heads_kv, draft_len, row_count // draft_len, head_dim).transpose(
        1, 0, 2, 3
    )
    return result.reshape(draft_len, heads_kv * row_count // draft_len * head_dim).astype(
        jnp.bfloat16
    )


def body(
    draft_states,
    w_qkv,
    w_out,
    kv_pool,
    resident_kv,
    page_owner,
    page_slot,
    hist_len,
    res_count,
    parents,
    ring,
):
    pool_size = lax.axis_size("pool")
    my_index = lax.axis_index("pool")
    group_size = H // KVH
    local_cols = w_qkv.shape[1]
    heads_kv = local_cols // ((group_size + 2) * HD)
    projected = lax.psum_scatter(
        jnp.dot(draft_states, w_qkv, preferred_element_type=jnp.float32),
        "pool",
        scatter_dimension=0,
        tiled=True,
    )
    projected = projected.reshape(USER_DEV, DRAFT, heads_kv, group_size + 2, HD)
    first_user = my_index * USER_DEV
    my_lengths = lax.dynamic_slice_in_dim(hist_len, first_user, USER_DEV)
    my_resident = lax.dynamic_slice_in_dim(res_count, first_user, USER_DEV)
    my_parents = lax.dynamic_slice_in_dim(parents, first_user, USER_DEV, 0)
    ancestry = ancestry_of(my_parents)
    positions = my_lengths.astype(jnp.float32)[:, None] + jnp.sum(ancestry, -1) - 1.0
    queries = rotate(projected[:, :, :, :group_size], positions[:, :, None, None]).astype(
        jnp.bfloat16
    )
    draft_key = rotate(projected[:, :, :, group_size], positions[:, :, None]).astype(jnp.bfloat16)
    draft_value = projected[:, :, :, group_size + 1].astype(jnp.bfloat16)
    row_count = DRAFT * group_size
    query_rows = queries.transpose(0, 2, 1, 3, 4).reshape(USER_DEV, heads_kv, row_count, HD)
    visible = jnp.repeat(ancestry > 0.5, group_size, axis=1)
    block_rows = USER_DEV * MAXP
    capacity = block_rows // pool_size
    kv_cols = kv_pool.shape[2]
    owner_blocks = page_owner.reshape(pool_size, block_rows)
    slot_blocks = page_slot.reshape(pool_size, block_rows)
    one_hot = (owner_blocks[:, :, None] == jnp.arange(pool_size)[None, None, :]).astype(jnp.int32)
    slot_ranks = jnp.sum((jnp.cumsum(one_hot, axis=1) - one_hot) * one_hot, axis=2)
    hot_owner = jnp.argmax(jnp.sum(one_hot, axis=1), axis=1)
    mine = owner_blocks == my_index
    targets = jnp.arange(pool_size)[:, None] * capacity + slot_ranks
    send_to = jnp.where(mine & (slot_ranks < capacity), targets, pool_size * capacity)
    pack_index = (
        jnp.zeros((pool_size * capacity,), jnp.int32)
        .at[send_to.reshape(-1)]
        .set(slot_blocks.reshape(-1), mode="drop")
    )
    extra_to = jnp.where(mine & (slot_ranks >= capacity), slot_ranks - capacity, capacity)
    extra_index = (
        jnp.zeros((capacity,), jnp.int32)
        .at[extra_to.reshape(-1)]
        .set(slot_blocks.reshape(-1), mode="drop")
    )
    piece_rows = capacity * PAGE // pool_size
    arrived = lax.all_to_all(
        kv_pool[pack_index], "pool", split_axis=0, concat_axis=0, tiled=True
    )
    spread = lax.all_to_all(
        kv_pool[extra_index].reshape(pool_size, piece_rows, kv_cols),
        "pool",
        split_axis=0,
        concat_axis=0,
        tiled=True,
    )
    extra = lax.all_to_all(
        spread[hot_owner], "pool", split_axis=0, concat_axis=0, tiled=True
    ).reshape(capacity, PAGE, kv_cols)
    local_source = resident_kv.reshape(USER_DEV * MAXRES, PAGE, kv_cols)
    outputs = []
    my_owner = lax.dynamic_index_in_dim(owner_blocks, my_index, 0, keepdims=False).reshape(
        USER_DEV, MAXP
    )
    my_rank = lax.dynamic_index_in_dim(slot_ranks, my_index, 0, keepdims=False).reshape(
        USER_DEV, MAXP
    )
    numbers = jnp.arange(MAXP)
    for local_user in range(USER_DEV):
        owner = my_owner[local_user]
        rank = my_rank[local_user]
        resident_pages = local_source[local_user * MAXRES + jnp.minimum(numbers, MAXRES - 1)]
        regular_pages = arrived[owner * capacity + jnp.minimum(rank, capacity - 1)]
        extra_pages = extra[jnp.clip(rank - capacity, 0, capacity - 1)]
        history = jnp.where(
            (numbers < my_resident[local_user])[:, None, None],
            resident_pages,
            jnp.where((rank < capacity)[:, None, None], regular_pages, extra_pages),
        ).reshape(MAXP * PAGE, kv_cols)
        result = attend_dense(
            query_rows[local_user],
            history,
            draft_key[local_user],
            draft_value[local_user],
            visible[local_user],
            my_lengths[local_user],
        )
        outputs.append(finish(result, DRAFT))
    attention = jnp.concatenate(outputs, 0)
    return halving_sum(ring_product(attention, w_out, "pool", ring), "tp").astype(jnp.bfloat16)


def ring_product(block, weights, axis_name, ring):
    count = len(ring)
    me = lax.axis_index(axis_name)
    ring_order = jnp.array(ring, jnp.int32)
    position = jnp.array([ring.index(index) for index in range(count)], jnp.int32)[me]
    forward = [(ring[k], ring[(k + 1) % count]) for k in range(count)]
    backward = [(ring[k], ring[(k - 1) % count]) for k in range(count)]
    product = jnp.zeros((count, block.shape[0], weights.shape[1]), jnp.float32)

    def place(product, rows, owner):
        return lax.dynamic_update_index_in_dim(
            product, jnp.dot(rows, weights, preferred_element_type=jnp.float32), owner, 0
        )

    product = place(product, block, me)
    ahead = block
    behind = block
    half = block.shape[0] // 2
    for step in range(1, count // 2 + 1):
        if step < count - step:
            ahead = lax.ppermute(ahead, axis_name, forward)
            product = place(product, ahead, ring_order[(position - step) % count])
            behind = lax.ppermute(behind, axis_name, backward)
            product = place(product, behind, ring_order[(position + step) % count])
        else:
            first = lax.ppermute(ahead[:half], axis_name, forward)
            second = lax.ppermute(behind[half:], axis_name, backward)
            product = place(
                product, jnp.concatenate([first, second], 0), ring_order[(position - step) % count]
            )
    return product.reshape(count * block.shape[0], weights.shape[1])


def grid_ring(mesh):
    count = mesh.shape["pool"]
    try:
        places = {}
        for index in range(count):
            device = mesh.devices[index, 0]
            places[(device.coords[2], device.coords[0])] = index
        rows = sorted({z for z, x in places})
        cols = sorted({x for z, x in places})
        if len(rows) % 2 or len(rows) * len(cols) != count or len(cols) < 2:
            return list(range(count))
        cycle = [places[(z, cols[0])] for z in rows]
        for k, z in enumerate(reversed(rows)):
            line = cols[1:] if k % 2 == 0 else cols[:0:-1]
            cycle += [places[(z, x)] for x in line]
        return cycle
    except (AttributeError, IndexError, KeyError, TypeError):
        return list(range(count))


def halving_sum(partial, axis_name):
    size = lax.axis_size(axis_name)
    me = lax.axis_index(axis_name)
    rows = partial.shape[0] // size
    cols = partial.shape[1]
    held = partial
    bit = 1
    while bit < size:
        blocks = held.shape[0] // rows
        grouped = held.reshape(blocks // 2, 2, rows, cols)
        mine = (me // bit) % 2
        keep = lax.dynamic_index_in_dim(grouped, mine, 1, keepdims=False)
        send = lax.dynamic_index_in_dim(grouped, 1 - mine, 1, keepdims=False)
        partners = [(j, j ^ bit) for j in range(size)]
        if bit > 1:
            send = send.astype(jnp.bfloat16)
            cut = send.shape[-1] // 2
            received = jnp.concatenate(
                [
                    lax.ppermute(send[..., :cut], axis_name, partners),
                    lax.ppermute(send[..., cut:], axis_name, partners),
                ],
                -1,
            )
        else:
            received = lax.ppermute(send, axis_name, partners)
        held = (keep + received.astype(jnp.float32)).reshape(blocks // 2 * rows, cols)
        bit *= 2
    return held


def solution(mesh):
    in_specs = (
        P(None, "pool"),
        P("pool", "tp"),
        P("tp", "pool"),
        P("pool", None, "tp"),
        P("pool", None, None, "tp"),
        P(),
        P(),
        P(),
        P(),
        P(),
    )
    out_specs = P("tp", "pool")
    return jax.shard_map(functools.partial(body, ring=grid_ring(mesh)), mesh=mesh, in_specs=in_specs, out_specs=out_specs, check_vma=False)
```

```python
import functools
import math

import jax
import jax.numpy as jnp
from jax import lax
from jax.sharding import PartitionSpec as P

H = 64
KVH = 8
HD = 128
DRAFT = 64
PAGE = 128
MAXP = 32
MAXRES = 8
USER_DEV = 2


ROPE_BASE = 500000.0


def ancestry_of(parents):
    users_count, draft_len = parents.shape
    tokens = jnp.arange(draft_len)
    reach = (parents[:, :, None] == tokens[None, None, :]).astype(jnp.float32)
    reach = reach + (tokens[:, None] == tokens[None, :]).astype(jnp.float32)[None]
    for unused in range(max(1, math.ceil(math.log2(draft_len)))):
        reach = jnp.minimum(
            jnp.einsum(
                "uij,ujk->uik",
                reach.astype(jnp.bfloat16),
                reach.astype(jnp.bfloat16),
                preferred_element_type=jnp.float32,
            ),
            1.0,
        )
    return reach


def rotate(vectors, positions):
    half_size = vectors.shape[-1] // 2
    frequencies = jnp.exp(
        jnp.arange(half_size).astype(jnp.float32) * (-2.0 * math.log(ROPE_BASE) / vectors.shape[-1])
    )
    angles = positions[..., None] * frequencies
    cosines = jnp.cos(angles)
    sines = jnp.sin(angles)
    lower_half = vectors[..., :half_size]
    upper_half = vectors[..., half_size:]
    return jnp.concatenate(
        [lower_half * cosines - upper_half * sines, upper_half * cosines + lower_half * sines], -1
    )


def attend_dense(queries, history, draft_key, draft_value, visible, length):
    heads_kv, row_count, head_dim = queries.shape
    score_scale = head_dim ** (-0.5)
    hist_ok = (jnp.arange(history.shape[0]) < length)[None, :]
    results = []
    for head in range(heads_kv):
        keys = history[:, 2 * head * head_dim : (2 * head + 1) * head_dim]
        values = history[:, (2 * head + 1) * head_dim : (2 * head + 2) * head_dim]
        hist_scores = (
            jnp.einsum("rd,sd->rs", queries[head], keys, preferred_element_type=jnp.float32)
            * score_scale
        )
        draft_scores = (
            jnp.einsum(
                "rd,jd->rj", queries[head], draft_key[:, head], preferred_element_type=jnp.float32
            )
            * score_scale
        )
        row_max = jnp.maximum(
            jnp.max(jnp.where(hist_ok, hist_scores, -jnp.inf), -1),
            jnp.max(jnp.where(visible, draft_scores, -jnp.inf), -1),
        )
        hist_weight = jnp.where(hist_ok, jnp.exp(hist_scores - row_max[:, None]), 0.0)
        draft_weight = jnp.where(visible, jnp.exp(draft_scores - row_max[:, None]), 0.0)
        denominator = jnp.sum(hist_weight, -1) + jnp.sum(draft_weight, -1)
        weighted = jnp.einsum(
            "rs,sd->rd",
            hist_weight.astype(jnp.bfloat16),
            values,
            preferred_element_type=jnp.float32,
        ) + jnp.einsum(
            "rj,jd->rd",
            draft_weight.astype(jnp.bfloat16),
            draft_value[:, head],
            preferred_element_type=jnp.float32,
        )
        results.append(weighted / denominator[:, None])
    return jnp.stack(results, 0)


def finish(result, draft_len):
    heads_kv, row_count, head_dim = result.shape
    result = result.reshape(heads_kv, draft_len, row_count // draft_len, head_dim).transpose(
        1, 0, 2, 3
    )
    return result.reshape(draft_len, heads_kv * row_count // draft_len * head_dim).astype(
        jnp.bfloat16
    )


def body(
    draft_states,
    w_qkv,
    w_out,
    kv_pool,
    resident_kv,
    page_owner,
    page_slot,
    hist_len,
    res_count,
    parents,
    ring,
):
    pool_size = lax.axis_size("pool")
    my_index = lax.axis_index("pool")
    group_size = H // KVH
    local_cols = w_qkv.shape[1]
    heads_kv = local_cols // ((group_size + 2) * HD)
    projected = lax.psum_scatter(
        jnp.dot(draft_states, w_qkv, preferred_element_type=jnp.float32),
        "pool",
        scatter_dimension=0,
        tiled=True,
    )
    projected = projected.reshape(USER_DEV, DRAFT, heads_kv, group_size + 2, HD)
    first_user = my_index * USER_DEV
    my_lengths = lax.dynamic_slice_in_dim(hist_len, first_user, USER_DEV)
    my_resident = lax.dynamic_slice_in_dim(res_count, first_user, USER_DEV)
    my_parents = lax.dynamic_slice_in_dim(parents, first_user, USER_DEV, 0)
    ancestry = ancestry_of(my_parents)
    positions = my_lengths.astype(jnp.float32)[:, None] + jnp.sum(ancestry, -1) - 1.0
    queries = rotate(projected[:, :, :, :group_size], positions[:, :, None, None]).astype(
        jnp.bfloat16
    )
    draft_key = rotate(projected[:, :, :, group_size], positions[:, :, None]).astype(jnp.bfloat16)
    draft_value = projected[:, :, :, group_size + 1].astype(jnp.bfloat16)
    row_count = DRAFT * group_size
    query_rows = queries.transpose(0, 2, 1, 3, 4).reshape(USER_DEV, heads_kv, row_count, HD)
    visible = jnp.repeat(ancestry > 0.5, group_size, axis=1)
    block_rows = USER_DEV * MAXP
    capacity = block_rows // pool_size
    kv_cols = kv_pool.shape[2]
    owner_blocks = page_owner.reshape(pool_size, block_rows)
    slot_blocks = page_slot.reshape(pool_size, block_rows)
    one_hot = (owner_blocks[:, :, None] == jnp.arange(pool_size)[None, None, :]).astype(jnp.int32)
    slot_ranks = jnp.sum((jnp.cumsum(one_hot, axis=1) - one_hot) * one_hot, axis=2)
    hot_owner = jnp.argmax(jnp.sum(one_hot, axis=1), axis=1)
    mine = owner_blocks == my_index
    targets = jnp.arange(pool_size)[:, None] * capacity + slot_ranks
    send_to = jnp.where(mine & (slot_ranks < capacity), targets, pool_size * capacity)
    pack_index = (
        jnp.zeros((pool_size * capacity,), jnp.int32)
        .at[send_to.reshape(-1)]
        .set(slot_blocks.reshape(-1), mode="drop")
    )
    extra_to = jnp.where(mine & (slot_ranks >= capacity), slot_ranks - capacity, capacity)
    extra_index = (
        jnp.zeros((capacity,), jnp.int32)
        .at[extra_to.reshape(-1)]
        .set(slot_blocks.reshape(-1), mode="drop")
    )
    piece_rows = capacity * PAGE // pool_size
    arrived = lax.all_to_all(
        kv_pool[pack_index], "pool", split_axis=0, concat_axis=0, tiled=True
    )
    spread = lax.all_to_all(
        kv_pool[extra_index].reshape(pool_size, piece_rows, kv_cols),
        "pool",
        split_axis=0,
        concat_axis=0,
        tiled=True,
    )
    extra = lax.all_to_all(
        spread[hot_owner], "pool", split_axis=0, concat_axis=0, tiled=True
    ).reshape(capacity, PAGE, kv_cols)
    local_source = resident_kv.reshape(USER_DEV * MAXRES, PAGE, kv_cols)
    outputs = []
    my_owner = lax.dynamic_index_in_dim(owner_blocks, my_index, 0, keepdims=False).reshape(
        USER_DEV, MAXP
    )
    my_rank = lax.dynamic_index_in_dim(slot_ranks, my_index, 0, keepdims=False).reshape(
        USER_DEV, MAXP
    )
    numbers = jnp.arange(MAXP)
    for local_user in range(USER_DEV):
        owner = my_owner[local_user]
        rank = my_rank[local_user]
        resident_pages = local_source[local_user * MAXRES + jnp.minimum(numbers, MAXRES - 1)]
        regular_pages = arrived[owner * capacity + jnp.minimum(rank, capacity - 1)]
        extra_pages = extra[jnp.clip(rank - capacity, 0, capacity - 1)]
        history = jnp.where(
            (numbers < my_resident[local_user])[:, None, None],
            resident_pages,
            jnp.where((rank < capacity)[:, None, None], regular_pages, extra_pages),
        ).reshape(MAXP * PAGE, kv_cols)
        result = attend_dense(
            query_rows[local_user],
            history,
            draft_key[local_user],
            draft_value[local_user],
            visible[local_user],
            my_lengths[local_user],
        )
        outputs.append(finish(result, DRAFT))
    attention = jnp.concatenate(outputs, 0)
    return halving_sum(ring_product(attention, w_out, "pool", ring), "tp").astype(jnp.bfloat16)


def ring_product(block, weights, axis_name, ring):
    count = len(ring)
    me = lax.axis_index(axis_name)
    ring_order = jnp.array(ring, jnp.int32)
    position = jnp.array([ring.index(index) for index in range(count)], jnp.int32)[me]
    forward = [(ring[k], ring[(k + 1) % count]) for k in range(count)]
    backward = [(ring[k], ring[(k - 1) % count]) for k in range(count)]
    product = jnp.zeros((count, block.shape[0], weights.shape[1]), jnp.float32)

    def place(product, rows, owner):
        return lax.dynamic_update_index_in_dim(
            product, jnp.dot(rows, weights, preferred_element_type=jnp.float32), owner, 0
        )

    product = place(product, block, me)
    ahead = block
    behind = block
    half = block.shape[0] // 2
    for step in range(1, count // 2 + 1):
        if step < count - step:
            ahead = lax.ppermute(ahead, axis_name, forward)
            product = place(product, ahead, ring_order[(position - step) % count])
            behind = lax.ppermute(behind, axis_name, backward)
            product = place(product, behind, ring_order[(position + step) % count])
        else:
            first = lax.ppermute(ahead[:half], axis_name, forward)
            second = lax.ppermute(behind[half:], axis_name, backward)
            product = place(
                product, jnp.concatenate([first, second], 0), ring_order[(position - step) % count]
            )
    return product.reshape(count * block.shape[0], weights.shape[1])


def grid_ring(mesh):
    count = mesh.shape["pool"]
    try:
        places = {}
        for index in range(count):
            device = mesh.devices[index, 0]
            places[(device.coords[2], device.coords[0])] = index
        rows = sorted({z for z, x in places})
        cols = sorted({x for z, x in places})
        if len(rows) % 2 or len(rows) * len(cols) != count or len(cols) < 2:
            return list(range(count))
        cycle = [places[(z, cols[0])] for z in rows]
        for k, z in enumerate(reversed(rows)):
            line = cols[1:] if k % 2 == 0 else cols[:0:-1]
            cycle += [places[(z, x)] for x in line]
        return cycle
    except (AttributeError, IndexError, KeyError, TypeError):
        return list(range(count))


def halving_sum(partial, axis_name):
    size = lax.axis_size(axis_name)
    me = lax.axis_index(axis_name)
    rows = partial.shape[0] // size
    cols = partial.shape[1]
    held = partial
    bit = 1
    while bit < size:
        blocks = held.shape[0] // rows
        grouped = held.reshape(blocks // 2, 2, rows, cols)
        mine = (me // bit) % 2
        keep = lax.dynamic_index_in_dim(grouped, mine, 1, keepdims=False)
        send = lax.dynamic_index_in_dim(grouped, 1 - mine, 1, keepdims=False)
        send = send.astype(jnp.bfloat16)
        received = lax.ppermute(send, axis_name, [(j, j ^ bit) for j in range(size)])
        held = (keep + received.astype(jnp.float32)).reshape(blocks // 2 * rows, cols)
        bit *= 2
    return held


def solution(mesh):
    in_specs = (
        P(None, "pool"),
        P("pool", "tp"),
        P("tp", "pool"),
        P("pool", None, "tp"),
        P("pool", None, None, "tp"),
        P(),
        P(),
        P(),
        P(),
        P(),
    )
    out_specs = P("tp", "pool")
    return jax.shard_map(functools.partial(body, ring=grid_ring(mesh)), mesh=mesh, in_specs=in_specs, out_specs=out_specs, check_vma=False)
```
